128 devices in a mesh: dp: 4 (over z), fsdp: 32 (over x, y, core).
Axes of the slice: x: 4, y: 4, z: 4, core: 2. Of those that a mesh axis runs over, the one named last changes fastest.
Arguments:
- frames: bfloat16 [131072, 1024], P(('dp', 'fsdp')), may hold values from -6 to 6
- llm_grad: bfloat16 [131072, 1024], P(('dp', 'fsdp')), may hold values from -6 to 6
- dest_rank: int32 [128, 128], P(('dp', 'fsdp')), may hold values from 0 to 127, as said below
- utt_lengths: int32 [128, 4], P(('dp', 'fsdp')), may hold values from 1 to 512, 1024 in all within a row
- valid: int32 [131072], P(('dp', 'fsdp')), may hold values 0 or 1
- norm_gain: float32 [1024], replicated, may hold values from 0.25 to 1.75
- up_weight: bfloat16 [1024, 2048], P('fsdp'), may hold values from -0.1875 to 0.1875
- kernel: float32 [9, 1024], replicated, may hold values from -2 to 2
- down_weight: bfloat16 [1024, 1024], P('fsdp'), may hold values from -0.1875 to 0.1875
Outputs:
- input_grad: bfloat16 [131072, 1024], P(('dp', 'fsdp'))
- up_grad: float32 [1024, 2048], P('fsdp')
- down_grad: float32 [1024, 1024], P('fsdp')
- kernel_grad: float32 [9, 1024], replicated
- gain_grad: float32 [1024], replicated
The draws below stay inside these ranges and needn't reach their ends.
Inputs may be any that keep to these rules, and one draw needn't show every extreme that they name: `dest_rank`: each language-model rank sends its blocks in groups of 1 block, all of one group to one encoder rank and different groups to different ranks; every encoder block j is named by exactly one rank.
All inputs are finite; a program needn't handle non-finite values. No bound on the sum of `valid` on one device may be relied on, other than what follows from the above.
Results may differ from the reference program's by a relative error of at most 0.025.
Values may be sent and summed in bfloat16 or wider, within the bound.
No kernel may reach another device: no remote copies, remote signals or barrier semaphores. Data moves between devices by JAX's collectives and lax.ppermute only.
A program may use at most 256 MiB of HBM per device.

```python
import math
import jax
import jax.numpy as jnp
import numpy as np
from jax import lax

D = 1024
KER = 9
FR_DEV = 1024
CAPB = 1
UTT = 4
BLK = 8
ALL_FR = 131072
DEVICES = 128


def draw_dest_rank(key, part):
    ranks = DEVICES
    blocks_dev = FR_DEV // BLK
    groups = blocks_dev // CAPB
    key_outer, key_inner, key_offs = jax.random.split(key, 3)
    outer = jax.random.permutation(key_outer, ranks).astype(jnp.int32)
    inner = jax.random.permutation(key_inner, ranks).astype(jnp.int32)
    offsets = jax.random.permutation(key_offs, ranks).astype(jnp.int32)[:groups]
    group_of = jnp.arange(blocks_dev, dtype=jnp.int32) // CAPB
    spot = (inner[:, None] + offsets[group_of][None, :]) % ranks
    return outer[spot].astype(jnp.int32)


def touch_ends(entries, rng, low, high):
    longest = entries.shape.index(max(entries.shape))
    spots = []
    for shift in (0, 1):
        where = [jax.random.randint(jax.random.fold_in(rng, axis), (), 0, length) for axis, length in enumerate(entries.shape)]
        where[longest] = (where[longest] + shift) % entries.shape[longest]
        spots.append(tuple(where))
    return entries.at[spots[0]].set(low).at[spots[1]].set(high)


def levels(key, dims, cuts, low, top_value):
    gain = 1.0
    for axis_at, blocks in cuts:
        draws = jax.random.uniform(jax.random.fold_in(jax.random.fold_in(key, 6), axis_at), (blocks,), jnp.float32, low / len(cuts), top_value / len(cuts))
        gain = gain * jnp.repeat(jnp.exp(draws), dims[axis_at] // blocks).reshape((-1,) + (1,) * (len(dims) - 1 - axis_at))
    return gain


def split_up(number_of, total, bound, skew):
    loads = [(1 << 20) // math.isqrt(rank ** skew) + 1 for rank in range(2, number_of + 1)]
    spare, counts = total - bound - (number_of - 1), [1] * (number_of - 1)
    while spare > 0:
        free = [i for i in range(number_of - 1) if counts[i] < bound]
        pool, left = sum([loads[i] for i in free]), spare
        for i in free:
            more = min(bound - counts[i], max(1, left * loads[i] // pool), spare)
            counts[i] = counts[i] + more
            spare = spare - more
    return np.array([bound] + counts)


def uneven_parts(stream_key, number_of, total, most, slope):
    if number_of == 2:
        one = jax.random.randint(stream_key, (), max(1, total - most), min(most, total - 1) + 1)
        return jnp.stack([one, total - one])
    sizes = jnp.asarray(split_up(number_of, total, most, slope), jnp.int32)
    pairs = (number_of - 1) // 2
    giver, receiver = sizes[1:1 + 2 * pairs:2], sizes[2:2 + 2 * pairs:2]
    margin = jnp.minimum(giver - 1, most - receiver)
    passed = jax.random.randint(jax.random.fold_in(stream_key, 1), (pairs,), 0, 1 << 20) % (margin + 1)
    sizes = sizes.at[1:1 + 2 * pairs:2].set(giver - passed).at[2:2 + 2 * pairs:2].set(receiver + passed)
    return sizes[jax.random.permutation(jax.random.fold_in(stream_key, 2), number_of)]


def bell_draw(own_key, dims, deviation, most, cuts=(), held_as=jnp.bfloat16):
    array = deviation * jax.random.normal(own_key, dims, jnp.float32)
    if cuts:
        array = array * levels(own_key, dims, cuts, -0.22, 0.18)
    return jnp.clip(array, -most, most).astype(held_as)


def setup_inputs(seed: int = 0) -> dict:
    keys = jax.random.split(jax.random.key(seed), 10)
    return {
        "frames": bell_draw(keys[0], (ALL_FR, D), 1.0, 6.0, ((0, 128),)),
        "llm_grad": bell_draw(keys[1], (ALL_FR, D), 1.0, 6.0, ((0, 128),)),
        "dest_rank": draw_dest_rank(jax.random.fold_in(keys[9], 71), 0),
        "utt_lengths": jax.vmap(lambda own: uneven_parts(own, UTT, FR_DEV, FR_DEV // 2, 2))(jax.random.split(keys[3], DEVICES)).reshape((DEVICES, UTT)).astype(jnp.int32),
        "valid": touch_ends((jax.random.randint(keys[4], (ALL_FR,), 0, 8) < 7).astype(jnp.int32), jax.random.fold_in(keys[4], 1), 0, 1),
        "norm_gain": jnp.clip(1.0 + 0.15 * jax.random.normal(keys[5], (D,), jnp.float32), 0.25, 1.75),
        "up_weight": bell_draw(keys[6], (D, 2 * D), D ** -0.5, 0.1875, ((0, 32),)),
        "kernel": bell_draw(keys[7], (KER, D), KER ** -0.5, 2.0, (), jnp.float32),
        "down_weight": bell_draw(keys[8], (D, D), D ** -0.5, 0.1875, ((0, 32),)),
    }


def shift_rows(values, offset, fill):
    rows = values.shape[0]
    if offset == 0:
        return values
    pad = jnp.full((abs(offset),) + values.shape[1:], fill, values.dtype)
    if offset > 0:
        return jnp.concatenate([values[offset:], pad], axis=0)
    return jnp.concatenate([pad, values[:rows + offset]], axis=0)

def segment_of(lengths, rows):
    ends = jnp.cumsum(lengths)
    place = jnp.arange(rows, dtype=jnp.int32)
    return lax.optimization_barrier(jnp.sum((place[:, None] >= ends[None, :]).astype(jnp.int32), axis=1))

def contract_rows(left, right):
    return lax.dot_general(left, right, (((0,), (0,)), ((), ())), preferred_element_type=jnp.float32)

def device_pass(frames, out_grad, lengths, valid, norm_gain, up_weight, kernel, down_weight):
    rows, width = frames.shape
    taps = kernel.shape[0]
    middle = (taps - 1) // 2
    seg = segment_of(lengths, rows)
    xf = frames.astype(jnp.float32)
    mean = lax.optimization_barrier(jnp.mean(xf, axis=1, keepdims=True))
    var = lax.optimization_barrier(jnp.mean((xf - mean) ** 2, axis=1, keepdims=True))
    rstd = lax.rsqrt(var + 1e-05)
    normed = (xf - mean) * rstd
    hidden = (normed * norm_gain[None, :]).astype(jnp.bfloat16)
    up = jnp.dot(hidden, up_weight, preferred_element_type=jnp.float32)
    value = up[:, :width]
    sig_b = jax.nn.sigmoid(up[:, width:])
    glu = (value * sig_b).astype(jnp.bfloat16)
    glu_f = glu.astype(jnp.float32)
    keep = valid.astype(jnp.float32)[:, None]
    sames = []
    conv = jnp.zeros((rows, width), jnp.float32)
    for k in range(taps):
        offset = k - middle
        same = (shift_rows(seg, offset, -1) == seg).astype(jnp.float32)[:, None]
        sames.append(same)
        conv = conv + kernel[k][None, :] * shift_rows(glu_f, offset, 0.0) * same
    conv = conv * keep
    sig_c = jax.nn.sigmoid(conv)
    act = (conv * sig_c).astype(jnp.bfloat16)
    down_term = contract_rows(act, out_grad)
    act_grad = jnp.dot(out_grad, down_weight.T, preferred_element_type=jnp.float32)
    conv_grad = act_grad * sig_c * (1.0 + conv * (1.0 - sig_c)) * keep
    kernel_rows = []
    glu_grad = jnp.zeros((rows, width), jnp.float32)
    for k in range(taps):
        offset = k - middle
        masked = conv_grad * sames[k]
        kernel_rows.append(lax.optimization_barrier(jnp.sum(masked * shift_rows(glu_f, offset, 0.0), axis=0)))
        glu_grad = glu_grad + kernel[k][None, :] * shift_rows(masked, -offset, 0.0)
    kernel_term = jnp.stack(kernel_rows, axis=0)
    value_grad = glu_grad * sig_b
    gate_grad = glu_grad * value * sig_b * (1.0 - sig_b)
    up_out_grad = jnp.concatenate([value_grad, gate_grad], axis=1).astype(jnp.bfloat16)
    up_term = contract_rows(hidden, up_out_grad)
    hidden_grad = jnp.dot(up_out_grad, up_weight.T, preferred_element_type=jnp.float32)
    gain_term = lax.optimization_barrier(jnp.sum(hidden_grad * normed, axis=0))
    scaled = hidden_grad * norm_gain[None, :]
    input_grad = rstd * (scaled - lax.optimization_barrier(jnp.mean(scaled, axis=1, keepdims=True)) - normed * lax.optimization_barrier(jnp.mean(scaled * normed, axis=1, keepdims=True)))
    return (input_grad.astype(jnp.bfloat16), up_term, down_term, kernel_term, gain_term)

def reference(frames, llm_grad, dest_rank, utt_lengths, valid, norm_gain, up_weight, kernel, down_weight):
    ranks = dest_rank.shape[0]
    blocks_dev = dest_rank.shape[1]
    width = frames.shape[1]
    rows = frames.shape[0] // ranks
    block_rows = rows // blocks_dev
    blocks = llm_grad.reshape(ranks, blocks_dev, block_rows, width)
    slot = jnp.broadcast_to(jnp.arange(blocks_dev, dtype=jnp.int32)[None, :], (ranks, blocks_dev))
    routed = jnp.zeros_like(blocks).at[dest_rank, slot].set(blocks).reshape(ranks, rows, width)
    frames_dev = frames.reshape(ranks, rows, width)
    valid_dev = valid.reshape(ranks, rows)

    def step(carry, item):
        x_rows, g_rows, lengths, mask_rows = item
        dx, up_term, down_term, kernel_term, gain_term = device_pass(x_rows, g_rows, lengths, mask_rows, norm_gain, up_weight, kernel, down_weight)
        return ((carry[0] + up_term, carry[1] + down_term, carry[2] + kernel_term, carry[3] + gain_term), dx)
    init = (jnp.zeros((width, 2 * width), jnp.float32), jnp.zeros((width, width), jnp.float32), jnp.zeros(kernel.shape, jnp.float32), jnp.zeros((width,), jnp.float32))
    totals, input_grad = lax.scan(step, init, (frames_dev, routed, utt_lengths, valid_dev))
    return (input_grad.reshape(ranks * rows, width), totals[0], totals[1], totals[2], totals[3])
```

```python
import jax
import jax.numpy as jnp
from jax import lax
from jax.sharding import PartitionSpec as P

CAPB = 1


def shift_rows(values, offset, fill):
    rows = values.shape[0]
    if offset == 0:
        return values
    pad = jnp.full((abs(offset),) + values.shape[1:], fill, values.dtype)
    if offset > 0:
        return jnp.concatenate([values[offset:], pad], axis=0)
    return jnp.concatenate([pad, values[: rows + offset]], axis=0)


def segment_of(lengths, rows):
    ends = jnp.cumsum(lengths)
    place = jnp.arange(rows, dtype=jnp.int32)
    return jnp.sum((place[:, None] >= ends[None, :]).astype(jnp.int32), axis=1)


def contract_rows(left, right):
    return lax.dot_general(
        left, right, (((0,), (0,)), ((), ())), preferred_element_type=jnp.float32
    )


def butterfly(x, axis):
    size = lax.axis_size(axis)
    if size & (size - 1):
        return lax.psum(x, axis)
    m = 1
    while m < size:
        x = x + lax.ppermute(x, axis, [(i, i ^ m) for i in range(size)])
        m *= 2
    return x


def route(llm_grad, dest_rank, ranks):
    rows, width = llm_grad.shape
    blocks_dev = dest_rank.shape[1]
    block_rows = rows // blocks_dev
    targets = dest_rank[0]
    grad_blocks = llm_grad.reshape(blocks_dev, block_rows, width)
    tags = jnp.broadcast_to(
        (jnp.arange(blocks_dev, dtype=jnp.float32) + 1.0)[:, None, None], (blocks_dev, 1, width)
    ).astype(jnp.bfloat16)
    tagged = jnp.concatenate([grad_blocks, tags], axis=1)
    send_sel = (targets[None, :] == jnp.arange(ranks, dtype=jnp.int32)[:, None]).astype(jnp.bfloat16)
    outbox = jnp.einsum(
        "dj,jrc->drc", send_sel, tagged, preferred_element_type=jnp.float32
    ).astype(jnp.bfloat16)
    inbox = lax.all_to_all(outbox, ("dp", "fsdp"), split_axis=0, concat_axis=0, tiled=True)
    tag_in = inbox[:, block_rows, 0].astype(jnp.float32)
    recv_sel = (
        tag_in[None, :] == (jnp.arange(blocks_dev, dtype=jnp.float32) + 1.0)[:, None]
    ).astype(jnp.bfloat16)
    placed = jnp.einsum(
        "js,src->jrc", recv_sel, inbox[:, :block_rows, :], preferred_element_type=jnp.float32
    ).astype(jnp.bfloat16)
    return placed.reshape(rows, width)


def on_device(
    frames, llm_grad, dest_rank, utt_lengths, valid, norm_gain, up_weight, kernel, down_weight
):
    rows, width = frames.shape
    n_data = lax.axis_size("dp")
    n_shard = lax.axis_size("fsdp")
    ranks = n_data * n_shard
    out_grad = route(llm_grad, dest_rank, ranks)
    up_full = lax.all_gather(up_weight, "fsdp", axis=0, tiled=True)
    down_full = lax.all_gather(down_weight, "fsdp", axis=0, tiled=True)
    taps = kernel.shape[0]
    middle = (taps - 1) // 2
    seg = segment_of(utt_lengths[0], rows)
    xf = frames.astype(jnp.float32)
    mean = jnp.mean(xf, axis=1, keepdims=True)
    var = jnp.mean((xf - mean) ** 2, axis=1, keepdims=True)
    rstd = lax.rsqrt(var + 1e-05)
    normed = (xf - mean) * rstd
    hidden = (normed * norm_gain[None, :]).astype(jnp.bfloat16)
    up = jnp.dot(hidden, up_full, preferred_element_type=jnp.float32)
    value = up[:, :width]
    sig_b = jax.nn.sigmoid(up[:, width:])
    glu = (value * sig_b).astype(jnp.bfloat16)
    glu_f = glu.astype(jnp.float32)
    keep = valid.astype(jnp.float32)[:, None]
    sames = []
    conv = jnp.zeros((rows, width), jnp.float32)
    for k in range(taps):
        offset = k - middle
        same = (shift_rows(seg, offset, -1) == seg).astype(jnp.float32)[:, None]
        sames.append(same)
        conv = conv + kernel[k][None, :] * shift_rows(glu_f, offset, 0.0) * same
    conv = conv * keep
    sig_c = jax.nn.sigmoid(conv)
    act = (conv * sig_c).astype(jnp.bfloat16)
    act_grad = jnp.dot(out_grad, down_full.T, preferred_element_type=jnp.float32)
    conv_grad = act_grad * sig_c * (1.0 + conv * (1.0 - sig_c)) * keep
    kernel_rows = []
    glu_grad = jnp.zeros((rows, width), jnp.float32)
    for k in range(taps):
        offset = k - middle
        masked = conv_grad * sames[k]
        kernel_rows.append(jnp.sum(masked * shift_rows(glu_f, offset, 0.0), axis=0))
        glu_grad = glu_grad + kernel[k][None, :] * shift_rows(masked, -offset, 0.0)
    kernel_term = jnp.stack(kernel_rows, axis=0)
    value_grad = glu_grad * sig_b
    gate_grad = glu_grad * value * sig_b * (1.0 - sig_b)
    up_out_grad = jnp.concatenate([value_grad, gate_grad], axis=1).astype(jnp.bfloat16)
    hidden_grad = jnp.dot(up_out_grad, up_full.T, preferred_element_type=jnp.float32)
    gain_term = jnp.sum(hidden_grad * normed, axis=0)
    scaled = hidden_grad * norm_gain[None, :]
    input_grad = rstd * (
        scaled
        - jnp.mean(scaled, axis=1, keepdims=True)
        - normed * jnp.mean(scaled * normed, axis=1, keepdims=True)
    )
    shard_sum = lax.psum_scatter(
        jnp.concatenate(
            [contract_rows(hidden, up_out_grad), contract_rows(act, out_grad)], axis=1
        ).astype(jnp.bfloat16),
        "fsdp",
        scatter_dimension=0,
        tiled=True,
    ).astype(jnp.float32)
    shard_sum = butterfly(shard_sum, "dp")
    small = jnp.concatenate([kernel_term, gain_term[None, :]], axis=0)
    small = butterfly(butterfly(small, "fsdp"), "dp")
    return (
        input_grad.astype(jnp.bfloat16),
        shard_sum[:, : 2 * width],
        shard_sum[:, 2 * width :],
        small[:taps],
        small[taps],
    )


def solution(mesh):
    return jax.shard_map(
        on_device,
        mesh=mesh,
        in_specs=(
            P(("dp", "fsdp"), None),
            P(("dp", "fsdp"), None),
            P(("dp", "fsdp"), None),
            P(("dp", "fsdp"), None),
            P(("dp", "fsdp")),
            P(),
            P("fsdp", None),
            P(),
            P("fsdp", None),
        ),
        out_specs=(P(("dp", "fsdp"), None), P("fsdp", None), P("fsdp", None), P(), P()),
        check_vma=False,
    )
```

```python
import jax
import jax.numpy as jnp
from jax import lax
from jax.sharding import PartitionSpec as P

CAPB = 1


def shift_rows(values, offset, fill):
    rows = values.shape[0]
    if offset == 0:
        return values
    pad = jnp.full((abs(offset),) + values.shape[1:], fill, values.dtype)
    if offset > 0:
        return jnp.concatenate([values[offset:], pad], axis=0)
    return jnp.concatenate([pad, values[: rows + offset]], axis=0)


def segment_of(lengths, rows):
    ends = jnp.cumsum(lengths)
    place = jnp.arange(rows, dtype=jnp.int32)
    return jnp.sum((place[:, None] >= ends[None, :]).astype(jnp.int32), axis=1)


def contract_rows(left, right):
    return lax.dot_general(
        left, right, (((0,), (0,)), ((), ())), preferred_element_type=jnp.float32
    )


def group_sum(x, axis):
    size = lax.axis_size(axis)
    if size & (size - 1):
        return lax.psum(x, axis)
    bits = size.bit_length() - 1
    shift = 0
    me = lax.axis_index(axis)
    while shift < bits:
        width = 1 if (shift == 0 and bits % 2) else 2
        n = 1 << width
        got = [x] + [
            lax.ppermute(x, axis, [(i, i ^ (d << shift)) for i in range(size)]) for d in range(1, n)
        ]
        stack = jnp.stack(got)
        mine = (me >> shift) & (n - 1)
        total = stack[mine]
        for m in range(1, n):
            total = total + stack[m ^ mine]
        x = total
        shift += width
    return x


def route(llm_grad, dest_rank, ranks):
    rows, width = llm_grad.shape
    blocks_dev = dest_rank.shape[1]
    block_rows = rows // blocks_dev
    targets = dest_rank[0]
    grad_blocks = llm_grad.reshape(blocks_dev, block_rows, width)
    tags = jnp.broadcast_to(
        (jnp.arange(blocks_dev, dtype=jnp.float32) + 1.0)[:, None, None], (blocks_dev, 1, width)
    ).astype(jnp.bfloat16)
    tagged = jnp.concatenate([grad_blocks, tags], axis=1)
    send_sel = (targets[None, :] == jnp.arange(ranks, dtype=jnp.int32)[:, None]).astype(jnp.bfloat16)
    outbox = jnp.einsum(
        "dj,jrc->drc", send_sel, tagged, preferred_element_type=jnp.float32
    ).astype(jnp.bfloat16)
    inbox = lax.all_to_all(outbox, ("dp", "fsdp"), split_axis=0, concat_axis=0, tiled=True)
    tag_in = inbox[:, block_rows, 0].astype(jnp.float32)
    recv_sel = (
        tag_in[None, :] == (jnp.arange(blocks_dev, dtype=jnp.float32) + 1.0)[:, None]
    ).astype(jnp.bfloat16)
    placed = jnp.einsum(
        "js,src->jrc", recv_sel, inbox[:, :block_rows, :], preferred_element_type=jnp.float32
    ).astype(jnp.bfloat16)
    return placed.reshape(rows, width)


def on_device(
    frames, llm_grad, dest_rank, utt_lengths, valid, norm_gain, up_weight, kernel, down_weight
):
    rows, width = frames.shape
    n_data = lax.axis_size("dp")
    n_shard = lax.axis_size("fsdp")
    ranks = n_data * n_shard
    up_full = lax.all_gather(up_weight, "fsdp", axis=0, tiled=True)
    llm_grad, up_full = lax.optimization_barrier((llm_grad, up_full))
    out_grad = route(llm_grad, dest_rank, ranks)
    down_full = lax.all_gather(down_weight, "fsdp", axis=0, tiled=True)
    taps = kernel.shape[0]
    middle = (taps - 1) // 2
    seg = segment_of(utt_lengths[0], rows)
    xf = frames.astype(jnp.float32)
    mean = jnp.mean(xf, axis=1, keepdims=True)
    var = jnp.mean((xf - mean) ** 2, axis=1, keepdims=True)
    rstd = lax.rsqrt(var + 1e-05)
    normed = (xf - mean) * rstd
    hidden = (normed * norm_gain[None, :]).astype(jnp.bfloat16)
    up = jnp.dot(hidden, up_full, preferred_element_type=jnp.float32)
    value = up[:, :width]
    sig_b = jax.nn.sigmoid(up[:, width:])
    glu = (value * sig_b).astype(jnp.bfloat16)
    glu_f = glu.astype(jnp.float32)
    keep = valid.astype(jnp.float32)[:, None]
    sames = []
    conv = jnp.zeros((rows, width), jnp.float32)
    for k in range(taps):
        offset = k - middle
        same = (shift_rows(seg, offset, -1) == seg).astype(jnp.float32)[:, None]
        sames.append(same)
        conv = conv + kernel[k][None, :] * shift_rows(glu_f, offset, 0.0) * same
    conv = conv * keep
    sig_c = jax.nn.sigmoid(conv)
    act = (conv * sig_c).astype(jnp.bfloat16)
    act_grad = jnp.dot(out_grad, down_full.T, preferred_element_type=jnp.float32)
    conv_grad = act_grad * sig_c * (1.0 + conv * (1.0 - sig_c)) * keep
    kernel_rows = []
    glu_grad = jnp.zeros((rows, width), jnp.float32)
    for k in range(taps):
        offset = k - middle
        masked = conv_grad * sames[k]
        kernel_rows.append(jnp.sum(masked * shift_rows(glu_f, offset, 0.0), axis=0))
        glu_grad = glu_grad + kernel[k][None, :] * shift_rows(masked, -offset, 0.0)
    kernel_term = jnp.stack(kernel_rows, axis=0)
    value_grad = glu_grad * sig_b
    gate_grad = glu_grad * value * sig_b * (1.0 - sig_b)
    up_out_grad = jnp.concatenate([value_grad, gate_grad], axis=1).astype(jnp.bfloat16)
    down_sum = lax.psum_scatter(
        contract_rows(act, out_grad).astype(jnp.bfloat16), "fsdp", scatter_dimension=0, tiled=True
    )
    up_out_grad, down_sum = lax.optimization_barrier((up_out_grad, down_sum))
    hidden_grad = jnp.dot(up_out_grad, up_full.T, preferred_element_type=jnp.float32)
    gain_term = jnp.sum(hidden_grad * normed, axis=0)
    small = group_sum(jnp.concatenate([kernel_term, gain_term[None, :]], axis=0), "fsdp")
    small = group_sum(small, "dp")
    scaled = hidden_grad * norm_gain[None, :]
    input_grad = rstd * (
        scaled
        - jnp.mean(scaled, axis=1, keepdims=True)
        - normed * jnp.mean(scaled * normed, axis=1, keepdims=True)
    )
    input_grad = input_grad.astype(jnp.bfloat16)
    up_term = contract_rows(hidden, up_out_grad).astype(jnp.bfloat16)
    up_term, small, input_grad = lax.optimization_barrier((up_term, small, input_grad))
    up_sum = lax.psum_scatter(up_term, "fsdp", scatter_dimension=0, tiled=True)
    shard_sum = jnp.concatenate([up_sum, down_sum], axis=1).astype(jnp.float32)
    shard_sum = group_sum(shard_sum, "dp")
    return (
        input_grad,
        shard_sum[:, : 2 * width],
        shard_sum[:, 2 * width :],
        small[:taps],
        small[taps],
    )


def solution(mesh):
    return jax.shard_map(
        on_device,
        mesh=mesh,
        in_specs=(
            P(("dp", "fsdp"), None),
            P(("dp", "fsdp"), None),
            P(("dp", "fsdp"), None),
            P(("dp", "fsdp"), None),
            P(("dp", "fsdp")),
            P(),
            P("fsdp", None),
            P(),
            P("fsdp", None),
        ),
        out_specs=(P(("dp", "fsdp"), None), P("fsdp", None), P("fsdp", None), P(), P()),
        check_vma=False,
    )
```

```python
import jax
import jax.numpy as jnp
from jax import lax
from jax.sharding import PartitionSpec as P

CAPB = 1


def shift_rows(values, offset, fill):
    rows = values.shape[0]
    if offset == 0:
        return values
    pad = jnp.full((abs(offset),) + values.shape[1:], fill, values.dtype)
    if offset > 0:
        return jnp.concatenate([values[offset:], pad], axis=0)
    return jnp.concatenate([pad, values[: rows + offset]], axis=0)


def segment_of(lengths, rows):
    ends = jnp.cumsum(lengths)
    place = jnp.arange(rows, dtype=jnp.int32)
    return jnp.sum((place[:, None] >= ends[None, :]).astype(jnp.int32), axis=1)


def contract_rows(left, right):
    return lax.dot_general(
        left, right, (((0,), (0,)), ((), ())), preferred_element_type=jnp.float32
    )


def butterfly(x, axis):
    size = lax.axis_size(axis)
    if size & (size - 1):
        return lax.psum(x, axis)
    m = 1
    while m < size:
        x = x + lax.ppermute(x, axis, [(i, i ^ m) for i in range(size)])
        m *= 2
    return x


def group_sum(x, axis):
    size = lax.axis_size(axis)
    if size & (size - 1):
        return lax.psum(x, axis)
    bits = size.bit_length() - 1
    shift = 0
    me = lax.axis_index(axis)
    while shift < bits:
        width = 1 if (shift == 0 and bits % 2) else 2
        n = 1 << width
        got = [x] + [
            lax.ppermute(x, axis, [(i, i ^ (d << shift)) for i in range(size)]) for d in range(1, n)
        ]
        stack = jnp.stack(got)
        mine = (me >> shift) & (n - 1)
        total = stack[mine]
        for m in range(1, n):
            total = total + stack[m ^ mine]
        x = total
        shift += width
    return x


def route(llm_grad, dest_rank, ranks):
    rows, width = llm_grad.shape
    blocks_dev = dest_rank.shape[1]
    block_rows = rows // blocks_dev
    targets = dest_rank[0]
    grad_blocks = llm_grad.reshape(blocks_dev, block_rows, width)
    tags = jnp.broadcast_to(
        (jnp.arange(blocks_dev, dtype=jnp.float32) + 1.0)[:, None, None], (blocks_dev, 1, width)
    ).astype(jnp.bfloat16)
    tagged = jnp.concatenate([grad_blocks, tags], axis=1)
    send_sel = (targets[None, :] == jnp.arange(ranks, dtype=jnp.int32)[:, None]).astype(jnp.bfloat16)
    outbox = jnp.einsum(
        "dj,jrc->drc", send_sel, tagged, preferred_element_type=jnp.float32
    ).astype(jnp.bfloat16)
    inbox = lax.all_to_all(outbox, ("dp", "fsdp"), split_axis=0, concat_axis=0, tiled=True)
    tag_in = inbox[:, block_rows, 0].astype(jnp.float32)
    recv_sel = (
        tag_in[None, :] == (jnp.arange(blocks_dev, dtype=jnp.float32) + 1.0)[:, None]
    ).astype(jnp.bfloat16)
    placed = jnp.einsum(
        "js,src->jrc", recv_sel, inbox[:, :block_rows, :], preferred_element_type=jnp.float32
    ).astype(jnp.bfloat16)
    return placed.reshape(rows, width)


def on_device(
    frames, llm_grad, dest_rank, utt_lengths, valid, norm_gain, up_weight, kernel, down_weight
):
    rows, width = frames.shape
    n_data = lax.axis_size("dp")
    n_shard = lax.axis_size("fsdp")
    ranks = n_data * n_shard
    out_grad = route(llm_grad, dest_rank, ranks)
    up_full = lax.all_gather(up_weight, "fsdp", axis=0, tiled=True)
    down_full = lax.all_gather(down_weight, "fsdp", axis=0, tiled=True)
    taps = kernel.shape[0]
    middle = (taps - 1) // 2
    seg = segment_of(utt_lengths[0], rows)
    xf = frames.astype(jnp.float32)
    mean = jnp.mean(xf, axis=1, keepdims=True)
    var = jnp.mean((xf - mean) ** 2, axis=1, keepdims=True)
    rstd = lax.rsqrt(var + 1e-05)
    normed = (xf - mean) * rstd
    hidden = (normed * norm_gain[None, :]).astype(jnp.bfloat16)
    up = jnp.dot(hidden, up_full, preferred_element_type=jnp.float32)
    value = up[:, :width]
    sig_b = jax.nn.sigmoid(up[:, width:])
    glu = (value * sig_b).astype(jnp.bfloat16)
    glu_f = glu.astype(jnp.float32)
    keep = valid.astype(jnp.float32)[:, None]
    sames = []
    conv = jnp.zeros((rows, width), jnp.float32)
    for k in range(taps):
        offset = k - middle
        same = (shift_rows(seg, offset, -1) == seg).astype(jnp.float32)[:, None]
        sames.append(same)
        conv = conv + kernel[k][None, :] * shift_rows(glu_f, offset, 0.0) * same
    conv = conv * keep
    sig_c = jax.nn.sigmoid(conv)
    act = (conv * sig_c).astype(jnp.bfloat16)
    act_grad = jnp.dot(out_grad, down_full.T, preferred_element_type=jnp.float32)
    conv_grad = act_grad * sig_c * (1.0 + conv * (1.0 - sig_c)) * keep
    glu_grad = jnp.zeros((rows, width), jnp.float32)
    for k in range(taps):
        offset = k - middle
        masked = conv_grad * sames[k]
        glu_grad = glu_grad + kernel[k][None, :] * shift_rows(masked, -offset, 0.0)
    value_grad = glu_grad * sig_b
    gate_grad = glu_grad * value * sig_b * (1.0 - sig_b)
    up_out_grad = jnp.concatenate([value_grad, gate_grad], axis=1).astype(jnp.bfloat16)
    weight_terms = jnp.concatenate(
        [contract_rows(hidden, up_out_grad), contract_rows(act, out_grad)], axis=1
    ).astype(jnp.bfloat16)
    weight_terms, conv_grad, up_out_grad = lax.optimization_barrier(
        (weight_terms, conv_grad, up_out_grad)
    )
    shard_sum = lax.psum_scatter(weight_terms, "fsdp", scatter_dimension=0, tiled=True)
    kernel_rows = []
    for k in range(taps):
        offset = k - middle
        masked = conv_grad * sames[k]
        kernel_rows.append(jnp.sum(masked * shift_rows(glu_f, offset, 0.0), axis=0))
    kernel_term = jnp.stack(kernel_rows, axis=0)
    hidden_grad = jnp.dot(up_out_grad, up_full.T, preferred_element_type=jnp.float32)
    gain_term = jnp.sum(hidden_grad * normed, axis=0)
    scaled = hidden_grad * norm_gain[None, :]
    input_grad = rstd * (
        scaled
        - jnp.mean(scaled, axis=1, keepdims=True)
        - normed * jnp.mean(scaled * normed, axis=1, keepdims=True)
    )
    small = jnp.concatenate([kernel_term, gain_term[None, :]], axis=0)
    small = group_sum(group_sum(small, "fsdp"), "dp")
    shard_sum = butterfly(shard_sum.astype(jnp.float32), "dp")
    return (
        input_grad.astype(jnp.bfloat16),
        shard_sum[:, : 2 * width],
        shard_sum[:, 2 * width :],
        small[:taps],
        small[taps],
    )


def solution(mesh):
    return jax.shard_map(
        on_device,
        mesh=mesh,
        in_specs=(
            P(("dp", "fsdp"), None),
            P(("dp", "fsdp"), None),
            P(("dp", "fsdp"), None),
            P(("dp", "fsdp"), None),
            P(("dp", "fsdp")),
            P(),
            P("fsdp", None),
            P(),
            P("fsdp", None),
        ),
        out_specs=(P(("dp", "fsdp"), None), P("fsdp", None), P("fsdp", None), P(), P()),
        check_vma=False,
    )
```

```python
import jax
import jax.numpy as jnp
from jax import lax
from jax.sharding import PartitionSpec as P

CAPB = 1


def shift_rows(values, offset, fill):
    rows = values.shape[0]
    if offset == 0:
        return values
    pad = jnp.full((abs(offset),) + values.shape[1:], fill, values.dtype)
    if offset > 0:
        return jnp.concatenate([values[offset:], pad], axis=0)
    return jnp.concatenate([pad, values[: rows + offset]], axis=0)


def segment_of(lengths, rows):
    ends = jnp.cumsum(lengths)
    place = jnp.arange(rows, dtype=jnp.int32)
    return jnp.sum((place[:, None] >= ends[None, :]).astype(jnp.int32), axis=1)


def contract_rows(left, right):
    return lax.dot_general(
        left, right, (((0,), (0,)), ((), ())), preferred_element_type=jnp.float32
    )


def butterfly(x, axis):
    size = lax.axis_size(axis)
    if size & (size - 1):
        return lax.psum(x, axis)
    m = 1
    while m < size:
        x = x + lax.ppermute(x, axis, [(i, i ^ m) for i in range(size)])
        m *= 2
    return x


def group_sum(x, axis):
    size = lax.axis_size(axis)
    if size & (size - 1):
        return lax.psum(x, axis)
    bits = size.bit_length() - 1
    shift = 0
    me = lax.axis_index(axis)
    while shift < bits:
        width = 1 if (shift == 0 and bits % 2) else 2
        n = 1 << width
        got = [x] + [
            lax.ppermute(x, axis, [(i, i ^ (d << shift)) for i in range(size)]) for d in range(1, n)
        ]
        stack = jnp.stack(got)
        mine = (me >> shift) & (n - 1)
        total = stack[mine]
        for m in range(1, n):
            total = total + stack[m ^ mine]
        x = total
        shift += width
    return x


def route(llm_grad, dest_rank, ranks):
    rows, width = llm_grad.shape
    blocks_dev = dest_rank.shape[1]
    block_rows = rows // blocks_dev
    targets = dest_rank[0]
    grad_blocks = llm_grad.reshape(blocks_dev, block_rows, width)
    tags = jnp.broadcast_to(
        (jnp.arange(blocks_dev, dtype=jnp.float32) + 1.0)[:, None, None], (blocks_dev, 1, width)
    ).astype(jnp.bfloat16)
    tagged = jnp.concatenate([grad_blocks, tags], axis=1)
    send_sel = (targets[None, :] == jnp.arange(ranks, dtype=jnp.int32)[:, None]).astype(jnp.bfloat16)
    outbox = jnp.einsum(
        "dj,jrc->drc", send_sel, tagged, preferred_element_type=jnp.float32
    ).astype(jnp.bfloat16)
    return outbox


def place(outbox, rows, width, blocks_dev):
    block_rows = rows // blocks_dev
    inbox = lax.all_to_all(outbox, ("dp", "fsdp"), split_axis=0, concat_axis=0, tiled=True)
    tag_in = inbox[:, block_rows, 0].astype(jnp.float32)
    recv_sel = (
        tag_in[None, :] == (jnp.arange(blocks_dev, dtype=jnp.float32) + 1.0)[:, None]
    ).astype(jnp.bfloat16)
    placed = jnp.einsum(
        "js,src->jrc", recv_sel, inbox[:, :block_rows, :], preferred_element_type=jnp.float32
    ).astype(jnp.bfloat16)
    return placed.reshape(rows, width)


def on_device(
    frames, llm_grad, dest_rank, utt_lengths, valid, norm_gain, up_weight, kernel, down_weight
):
    rows, width = frames.shape
    n_data = lax.axis_size("dp")
    n_shard = lax.axis_size("fsdp")
    ranks = n_data * n_shard
    up_full = lax.all_gather(up_weight, "fsdp", axis=0, tiled=True)
    llm_grad, up_full = lax.optimization_barrier((llm_grad, up_full))
    outbox = route(llm_grad, dest_rank, ranks)
    down_full = lax.all_gather(down_weight, "fsdp", axis=0, tiled=True)
    taps = kernel.shape[0]
    middle = (taps - 1) // 2
    seg = segment_of(utt_lengths[0], rows)
    xf = frames.astype(jnp.float32)
    mean = jnp.mean(xf, axis=1, keepdims=True)
    var = jnp.mean((xf - mean) ** 2, axis=1, keepdims=True)
    rstd = lax.rsqrt(var + 1e-05)
    normed = (xf - mean) * rstd
    hidden = (normed * norm_gain[None, :]).astype(jnp.bfloat16)
    hidden, up_full, outbox = lax.optimization_barrier((hidden, up_full, outbox))
    out_grad = place(outbox, rows, width, dest_rank.shape[1])
    up = jnp.dot(hidden, up_full, preferred_element_type=jnp.float32)
    value = up[:, :width]
    sig_b = jax.nn.sigmoid(up[:, width:])
    glu = (value * sig_b).astype(jnp.bfloat16)
    glu_f = glu.astype(jnp.float32)
    keep = valid.astype(jnp.float32)[:, None]
    sames = []
    conv = jnp.zeros((rows, width), jnp.float32)
    for k in range(taps):
        offset = k - middle
        same = (shift_rows(seg, offset, -1) == seg).astype(jnp.float32)[:, None]
        sames.append(same)
        conv = conv + kernel[k][None, :] * shift_rows(glu_f, offset, 0.0) * same
    conv = conv * keep
    sig_c = jax.nn.sigmoid(conv)
    act = (conv * sig_c).astype(jnp.bfloat16)
    act_grad = jnp.dot(out_grad, down_full.T, preferred_element_type=jnp.float32)
    conv_grad = act_grad * sig_c * (1.0 + conv * (1.0 - sig_c)) * keep
    glu_grad = jnp.zeros((rows, width), jnp.float32)
    for k in range(taps):
        offset = k - middle
        masked = conv_grad * sames[k]
        glu_grad = glu_grad + kernel[k][None, :] * shift_rows(masked, -offset, 0.0)
    value_grad = glu_grad * sig_b
    gate_grad = glu_grad * value * sig_b * (1.0 - sig_b)
    up_out_grad = jnp.concatenate([value_grad, gate_grad], axis=1).astype(jnp.bfloat16)
    weight_terms = jnp.concatenate(
        [contract_rows(hidden, up_out_grad), contract_rows(act, out_grad)], axis=1
    ).astype(jnp.bfloat16)
    weight_terms, conv_grad, up_out_grad = lax.optimization_barrier(
        (weight_terms, conv_grad, up_out_grad)
    )
    shard_sum = lax.psum_scatter(weight_terms, "fsdp", scatter_dimension=0, tiled=True)
    kernel_rows = []
    for k in range(taps):
        offset = k - middle
        masked = conv_grad * sames[k]
        kernel_rows.append(jnp.sum(masked * shift_rows(glu_f, offset, 0.0), axis=0))
    kernel_term = jnp.stack(kernel_rows, axis=0)
    hidden_grad = jnp.dot(up_out_grad, up_full.T, preferred_element_type=jnp.float32)
    gain_term = jnp.sum(hidden_grad * normed, axis=0)
    scaled = hidden_grad * norm_gain[None, :]
    input_grad = rstd * (
        scaled
        - jnp.mean(scaled, axis=1, keepdims=True)
        - normed * jnp.mean(scaled * normed, axis=1, keepdims=True)
    )
    small = jnp.concatenate([kernel_term, gain_term[None, :]], axis=0)
    small = group_sum(small, "fsdp")
    both = jnp.concatenate(
        [shard_sum.astype(jnp.float32), jnp.pad(small, ((0, 0), (0, 3 * width - small.shape[1])))],
        axis=0,
    )
    both = butterfly(both, "dp")
    shard_sum = both[: shard_sum.shape[0]]
    small = both[shard_sum.shape[0] :, :width]
    return (
        input_grad.astype(jnp.bfloat16),
        shard_sum[:, : 2 * width],
        shard_sum[:, 2 * width :],
        small[:taps],
        small[taps],
    )


def solution(mesh):
    return jax.shard_map(
        on_device,
        mesh=mesh,
        in_specs=(
            P(("dp", "fsdp"), None),
            P(("dp", "fsdp"), None),
            P(("dp", "fsdp"), None),
            P(("dp", "fsdp"), None),
            P(("dp", "fsdp")),
            P(),
            P("fsdp", None),
            P(),
            P("fsdp", None),
        ),
        out_specs=(P(("dp", "fsdp"), None), P("fsdp", None), P("fsdp", None), P(), P()),
        check_vma=False,
    )
```

```python
import jax
import jax.numpy as jnp
from jax import lax
from jax.sharding import PartitionSpec as P

CAPB = 1


def shift_rows(values, offset, fill):
    rows = values.shape[0]
    if offset == 0:
        return values
    pad = jnp.full((abs(offset),) + values.shape[1:], fill, values.dtype)
    if offset > 0:
        return jnp.concatenate([values[offset:], pad], axis=0)
    return jnp.concatenate([pad, values[: rows + offset]], axis=0)


def segment_of(lengths, rows):
    ends = jnp.cumsum(lengths)
    place = jnp.arange(rows, dtype=jnp.int32)
    return jnp.sum((place[:, None] >= ends[None, :]).astype(jnp.int32), axis=1)


def contract_rows(left, right):
    return lax.dot_general(
        left, right, (((0,), (0,)), ((), ())), preferred_element_type=jnp.float32
    )


def butterfly(x, axis):
    size = lax.axis_size(axis)
    if size & (size - 1):
        return lax.psum(x, axis)
    m = 1
    while m < size:
        x = x + lax.ppermute(x, axis, [(i, i ^ m) for i in range(size)])
        m *= 2
    return x


def group_sum(x, axis):
    size = lax.axis_size(axis)
    if size & (size - 1):
        return lax.psum(x, axis)
    bits = size.bit_length() - 1
    shift = 0
    me = lax.axis_index(axis)
    while shift < bits:
        width = 1 if (shift == 0 and bits % 2) else 2
        n = 1 << width
        got = [x] + [
            lax.ppermute(x, axis, [(i, i ^ (d << shift)) for i in range(size)]) for d in range(1, n)
        ]
        stack = jnp.stack(got)
        mine = (me >> shift) & (n - 1)
        total = stack[mine]
        for m in range(1, n):
            total = total + stack[m ^ mine]
        x = total
        shift += width
    return x


def route(llm_grad, dest_rank, ranks):
    rows, width = llm_grad.shape
    blocks_dev = dest_rank.shape[1]
    block_rows = rows // blocks_dev
    targets = dest_rank[0]
    grad_blocks = llm_grad.reshape(blocks_dev, block_rows, width)
    tags = jnp.broadcast_to(
        (jnp.arange(blocks_dev, dtype=jnp.float32) + 1.0)[:, None, None], (blocks_dev, 1, width)
    ).astype(jnp.bfloat16)
    tagged = jnp.concatenate([grad_blocks, tags], axis=1)
    send_sel = (targets[None, :] == jnp.arange(ranks, dtype=jnp.int32)[:, None]).astype(jnp.bfloat16)
    outbox = jnp.einsum(
        "dj,jrc->drc", send_sel, tagged, preferred_element_type=jnp.float32
    ).astype(jnp.bfloat16)
    inbox = lax.all_to_all(outbox, ("dp", "fsdp"), split_axis=0, concat_axis=0, tiled=True)
    tag_in = inbox[:, block_rows, 0].astype(jnp.float32)
    recv_sel = (
        tag_in[None, :] == (jnp.arange(blocks_dev, dtype=jnp.float32) + 1.0)[:, None]
    ).astype(jnp.bfloat16)
    placed = jnp.einsum(
        "js,src->jrc", recv_sel, inbox[:, :block_rows, :], preferred_element_type=jnp.float32
    ).astype(jnp.bfloat16)
    return placed.reshape(rows, width)


def on_device(
    frames, llm_grad, dest_rank, utt_lengths, valid, norm_gain, up_weight, kernel, down_weight
):
    rows, width = frames.shape
    n_data = lax.axis_size("dp")
    n_shard = lax.axis_size("fsdp")
    ranks = n_data * n_shard
    out_grad = route(llm_grad, dest_rank, ranks)
    up_full = lax.all_gather(up_weight, "fsdp", axis=0, tiled=True)
    down_full = lax.all_gather(down_weight, "fsdp", axis=0, tiled=True)
    taps = kernel.shape[0]
    middle = (taps - 1) // 2
    seg = segment_of(utt_lengths[0], rows)
    xf = frames.astype(jnp.float32)
    mean = jnp.mean(xf, axis=1, keepdims=True)
    var = jnp.mean((xf - mean) ** 2, axis=1, keepdims=True)
    rstd = lax.rsqrt(var + 1e-05)
    normed = (xf - mean) * rstd
    hidden = (normed * norm_gain[None, :]).astype(jnp.bfloat16)
    up = jnp.dot(hidden, up_full, preferred_element_type=jnp.float32)
    value = up[:, :width]
    sig_b = jax.nn.sigmoid(up[:, width:])
    glu = (value * sig_b).astype(jnp.bfloat16)
    glu_f = glu.astype(jnp.float32)
    keep = valid.astype(jnp.float32)[:, None]
    sames = []
    conv = jnp.zeros((rows, width), jnp.float32)
    for k in range(taps):
        offset = k - middle
        same = (shift_rows(seg, offset, -1) == seg).astype(jnp.float32)[:, None]
        sames.append(same)
        conv = conv + kernel[k][None, :] * shift_rows(glu_f, offset, 0.0) * same
    conv = conv * keep
    sig_c = jax.nn.sigmoid(conv)
    act = (conv * sig_c).astype(jnp.bfloat16)
    act_grad = jnp.dot(out_grad, down_full.T, preferred_element_type=jnp.float32)
    conv_grad = act_grad * sig_c * (1.0 + conv * (1.0 - sig_c)) * keep
    glu_grad = jnp.zeros((rows, width), jnp.float32)
    for k in range(taps):
        offset = k - middle
        masked = conv_grad * sames[k]
        glu_grad = glu_grad + kernel[k][None, :] * shift_rows(masked, -offset, 0.0)
    value_grad = glu_grad * sig_b
    gate_grad = glu_grad * value * sig_b * (1.0 - sig_b)
    up_out_grad = jnp.concatenate([value_grad, gate_grad], axis=1).astype(jnp.bfloat16)
    weight_terms = jnp.concatenate(
        [contract_rows(hidden, up_out_grad), contract_rows(act, out_grad)], axis=1
    ).astype(jnp.bfloat16)
    weight_terms, conv_grad, up_out_grad = lax.optimization_barrier(
        (weight_terms, conv_grad, up_out_grad)
    )
    shard_sum = lax.psum_scatter(weight_terms, "fsdp", scatter_dimension=0, tiled=True)
    kernel_rows = []
    for k in range(taps):
        offset = k - middle
        masked = conv_grad * sames[k]
        kernel_rows.append(jnp.sum(masked * shift_rows(glu_f, offset, 0.0), axis=0))
    kernel_term = jnp.stack(kernel_rows, axis=0)
    hidden_grad = jnp.dot(up_out_grad, up_full.T, preferred_element_type=jnp.float32)
    gain_term = jnp.sum(hidden_grad * normed, axis=0)
    scaled = hidden_grad * norm_gain[None, :]
    input_grad = rstd * (
        scaled
        - jnp.mean(scaled, axis=1, keepdims=True)
        - normed * jnp.mean(scaled * normed, axis=1, keepdims=True)
    )
    small = jnp.concatenate([kernel_term, gain_term[None, :]], axis=0)
    small = group_sum(small, "fsdp")
    both = jnp.concatenate(
        [shard_sum.astype(jnp.float32), jnp.pad(small, ((0, 0), (0, 3 * width - small.shape[1])))],
        axis=0,
    )
    both = butterfly(both, "dp")
    shard_sum = both[: shard_sum.shape[0]]
    small = both[shard_sum.shape[0] :, :width]
    return (
        input_grad.astype(jnp.bfloat16),
        shard_sum[:, : 2 * width],
        shard_sum[:, 2 * width :],
        small[:taps],
        small[taps],
    )


def solution(mesh):
    return jax.shard_map(
        on_device,
        mesh=mesh,
        in_specs=(
            P(("dp", "fsdp"), None),
            P(("dp", "fsdp"), None),
            P(("dp", "fsdp"), None),
            P(("dp", "fsdp"), None),
            P(("dp", "fsdp")),
            P(),
            P("fsdp", None),
            P(),
            P("fsdp", None),
        ),
        out_specs=(P(("dp", "fsdp"), None), P("fsdp", None), P("fsdp", None), P(), P()),
        check_vma=False,
    )
```

```python
import jax
import jax.numpy as jnp
from jax import lax
from jax.sharding import PartitionSpec as P

CAPB = 1


def shift_rows(values, offset, fill):
    rows = values.shape[0]
    if offset == 0:
        return values
    pad = jnp.full((abs(offset),) + values.shape[1:], fill, values.dtype)
    if offset > 0:
        return jnp.concatenate([values[offset:], pad], axis=0)
    return jnp.concatenate([pad, values[: rows + offset]], axis=0)


def segment_of(lengths, rows):
    ends = jnp.cumsum(lengths)
    place = jnp.arange(rows, dtype=jnp.int32)
    return jnp.sum((place[:, None] >= ends[None, :]).astype(jnp.int32), axis=1)


def contract_rows(left, right):
    return lax.dot_general(
        left, right, (((0,), (0,)), ((), ())), preferred_element_type=jnp.float32
    )


def butterfly(x, axis):
    size = lax.axis_size(axis)
    if size & (size - 1):
        return lax.psum(x, axis)
    m = 1
    while m < size:
        x = x + lax.ppermute(x, axis, [(i, i ^ m) for i in range(size)])
        m *= 2
    return x


def group_sum(x, axis):
    size = lax.axis_size(axis)
    if size & (size - 1):
        return lax.psum(x, axis)
    bits = size.bit_length() - 1
    shift = 0
    me = lax.axis_index(axis)
    while shift < bits:
        width = 1 if (shift == 0 and bits % 2) else 2
        n = 1 << width
        got = [x] + [
            lax.ppermute(x, axis, [(i, i ^ (d << shift)) for i in range(size)]) for d in range(1, n)
        ]
        stack = jnp.stack(got)
        mine = (me >> shift) & (n - 1)
        total = stack[mine]
        for m in range(1, n):
            total = total + stack[m ^ mine]
        x = total
        shift += width
    return x


def route(llm_grad, dest_rank, ranks):
    rows, width = llm_grad.shape
    blocks_dev = dest_rank.shape[1]
    block_rows = rows // blocks_dev
    lanes = 128
    col_tiles = width // lanes
    body = block_rows * col_tiles
    targets = dest_rank[0]
    grad_tiles = (
        llm_grad.reshape(blocks_dev, block_rows, col_tiles, lanes)
        .transpose(0, 2, 1, 3)
        .reshape(blocks_dev, body, lanes)
    )
    tags = jnp.broadcast_to(
        (jnp.arange(blocks_dev, dtype=jnp.float32) + 1.0)[:, None, None], (blocks_dev, 16, lanes)
    ).astype(jnp.bfloat16)
    tagged = jnp.concatenate([grad_tiles, tags], axis=1)
    send_sel = (targets[None, :] == jnp.arange(ranks, dtype=jnp.int32)[:, None]).astype(jnp.bfloat16)
    outbox = jnp.einsum(
        "dj,jqc->dqc", send_sel, tagged, preferred_element_type=jnp.float32
    ).astype(jnp.bfloat16)
    inbox = lax.all_to_all(outbox, ("dp", "fsdp"), split_axis=0, concat_axis=0, tiled=True)
    tag_in = inbox[:, body, 0].astype(jnp.float32)
    recv_sel = (
        tag_in[None, :] == (jnp.arange(blocks_dev, dtype=jnp.float32) + 1.0)[:, None]
    ).astype(jnp.bfloat16)
    placed = jnp.einsum(
        "js,sqc->jqc", recv_sel, inbox[:, :body, :], preferred_element_type=jnp.float32
    ).astype(jnp.bfloat16)
    return (
        placed.reshape(blocks_dev, col_tiles, block_rows, lanes)
        .transpose(0, 2, 1, 3)
        .reshape(rows, width)
    )


def on_device(
    frames, llm_grad, dest_rank, utt_lengths, valid, norm_gain, up_weight, kernel, down_weight
):
    rows, width = frames.shape
    n_data = lax.axis_size("dp")
    n_shard = lax.axis_size("fsdp")
    ranks = n_data * n_shard
    out_grad = route(llm_grad, dest_rank, ranks)
    up_full = lax.all_gather(up_weight, "fsdp", axis=0, tiled=True)
    down_full = lax.all_gather(down_weight, "fsdp", axis=0, tiled=True)
    taps = kernel.shape[0]
    middle = (taps - 1) // 2
    seg = segment_of(utt_lengths[0], rows)
    xf = frames.astype(jnp.float32)
    mean = jnp.mean(xf, axis=1, keepdims=True)
    var = jnp.mean((xf - mean) ** 2, axis=1, keepdims=True)
    rstd = lax.rsqrt(var + 1e-05)
    normed = (xf - mean) * rstd
    hidden = (normed * norm_gain[None, :]).astype(jnp.bfloat16)
    up = jnp.dot(hidden, up_full, preferred_element_type=jnp.float32)
    value = up[:, :width]
    sig_b = jax.nn.sigmoid(up[:, width:])
    glu = (value * sig_b).astype(jnp.bfloat16)
    glu_f = glu.astype(jnp.float32)
    keep = valid.astype(jnp.float32)[:, None]
    sames = []
    conv = jnp.zeros((rows, width), jnp.float32)
    for k in range(taps):
        offset = k - middle
        same = (shift_rows(seg, offset, -1) == seg).astype(jnp.float32)[:, None]
        sames.append(same)
        conv = conv + kernel[k][None, :] * shift_rows(glu_f, offset, 0.0) * same
    conv = conv * keep
    sig_c = jax.nn.sigmoid(conv)
    act = (conv * sig_c).astype(jnp.bfloat16)
    act_grad = jnp.dot(out_grad, down_full.T, preferred_element_type=jnp.float32)
    conv_grad = act_grad * sig_c * (1.0 + conv * (1.0 - sig_c)) * keep
    glu_grad = jnp.zeros((rows, width), jnp.float32)
    for k in range(taps):
        offset = k - middle
        masked = conv_grad * sames[k]
        glu_grad = glu_grad + kernel[k][None, :] * shift_rows(masked, -offset, 0.0)
    value_grad = glu_grad * sig_b
    gate_grad = glu_grad * value * sig_b * (1.0 - sig_b)
    up_out_grad = jnp.concatenate([value_grad, gate_grad], axis=1).astype(jnp.bfloat16)
    weight_terms = jnp.concatenate(
        [contract_rows(hidden, up_out_grad), contract_rows(act, out_grad)], axis=1
    ).astype(jnp.bfloat16)
    weight_terms, conv_grad, up_out_grad = lax.optimization_barrier(
        (weight_terms, conv_grad, up_out_grad)
    )
    shard_sum = lax.psum_scatter(weight_terms, "fsdp", scatter_dimension=0, tiled=True)
    kernel_rows = []
    for k in range(taps):
        offset = k - middle
        masked = conv_grad * sames[k]
        kernel_rows.append(jnp.sum(masked * shift_rows(glu_f, offset, 0.0), axis=0))
    kernel_term = jnp.stack(kernel_rows, axis=0)
    hidden_grad = jnp.dot(up_out_grad, up_full.T, preferred_element_type=jnp.float32)
    gain_term = jnp.sum(hidden_grad * normed, axis=0)
    scaled = hidden_grad * norm_gain[None, :]
    input_grad = rstd * (
        scaled
        - jnp.mean(scaled, axis=1, keepdims=True)
        - normed * jnp.mean(scaled * normed, axis=1, keepdims=True)
    )
    small = jnp.concatenate([kernel_term, gain_term[None, :]], axis=0)
    small = group_sum(group_sum(small, "fsdp"), "dp")
    shard_sum = butterfly(shard_sum.astype(jnp.float32), "dp")
    return (
        input_grad.astype(jnp.bfloat16),
        shard_sum[:, : 2 * width],
        shard_sum[:, 2 * width :],
        small[:taps],
        small[taps],
    )


def solution(mesh):
    return jax.shard_map(
        on_device,
        mesh=mesh,
        in_specs=(
            P(("dp", "fsdp"), None),
            P(("dp", "fsdp"), None),
            P(("dp", "fsdp"), None),
            P(("dp", "fsdp"), None),
            P(("dp", "fsdp")),
            P(),
            P("fsdp", None),
            P(),
            P("fsdp", None),
        ),
        out_specs=(P(("dp", "fsdp"), None), P("fsdp", None), P("fsdp", None), P(), P()),
        check_vma=False,
    )
```

```python
import jax
import jax.numpy as jnp
from jax import lax
from jax.sharding import PartitionSpec as P

CAPB = 1


def shift_rows(values, offset, fill):
    rows = values.shape[0]
    if offset == 0:
        return values
    pad = jnp.full((abs(offset),) + values.shape[1:], fill, values.dtype)
    if offset > 0:
        return jnp.concatenate([values[offset:], pad], axis=0)
    return jnp.concatenate([pad, values[: rows + offset]], axis=0)


def segment_of(lengths, rows):
    ends = jnp.cumsum(lengths)
    place = jnp.arange(rows, dtype=jnp.int32)
    return jnp.sum((place[:, None] >= ends[None, :]).astype(jnp.int32), axis=1)


def contract_rows(left, right):
    return lax.dot_general(
        left, right, (((0,), (0,)), ((), ())), preferred_element_type=jnp.float32
    )


def butterfly(x, axis):
    size = lax.axis_size(axis)
    if size & (size - 1):
        return lax.psum(x, axis)
    m = 1
    while m < size:
        x = x + lax.ppermute(x, axis, [(i, i ^ m) for i in range(size)])
        m *= 2
    return x


def group_sum(x, axis):
    size = lax.axis_size(axis)
    if size & (size - 1):
        return lax.psum(x, axis)
    bits = size.bit_length() - 1
    shift = 0
    me = lax.axis_index(axis)
    while shift < bits:
        width = 1 if (shift == 0 and bits % 2) else 2
        n = 1 << width
        got = [x] + [
            lax.ppermute(x, axis, [(i, i ^ (d << shift)) for i in range(size)]) for d in range(1, n)
        ]
        stack = jnp.stack(got)
        mine = (me >> shift) & (n - 1)
        total = stack[mine]
        for m in range(1, n):
            total = total + stack[m ^ mine]
        x = total
        shift += width
    return x


def route(llm_grad, dest_rank, ranks):
    rows, width = llm_grad.shape
    blocks_dev = dest_rank.shape[1]
    block_rows = rows // blocks_dev
    lanes = 128
    col_tiles = width // lanes
    body = block_rows * col_tiles
    targets = dest_rank[0]
    grad_tiles = (
        llm_grad.reshape(blocks_dev, block_rows, col_tiles, lanes)
        .transpose(0, 2, 1, 3)
        .reshape(blocks_dev, body, lanes)
    )
    tags = jnp.broadcast_to(
        (jnp.arange(blocks_dev, dtype=jnp.float32) + 1.0)[:, None, None], (blocks_dev, 16, lanes)
    ).astype(jnp.bfloat16)
    tagged = jnp.concatenate([grad_tiles, tags], axis=1)
    send_sel = (targets[None, :] == jnp.arange(ranks, dtype=jnp.int32)[:, None]).astype(jnp.bfloat16)
    outbox = jnp.einsum(
        "dj,jqc->dqc", send_sel, tagged, preferred_element_type=jnp.float32
    ).astype(jnp.bfloat16)
    inbox = lax.all_to_all(outbox, ("dp", "fsdp"), split_axis=0, concat_axis=0, tiled=True)
    tag_in = inbox[:, body, 0].astype(jnp.float32)
    recv_sel = (
        tag_in[None, :] == (jnp.arange(blocks_dev, dtype=jnp.float32) + 1.0)[:, None]
    ).astype(jnp.bfloat16)
    placed = jnp.einsum(
        "js,sqc->jqc", recv_sel, inbox[:, :body, :], preferred_element_type=jnp.float32
    ).astype(jnp.bfloat16)
    return (
        placed.reshape(blocks_dev, col_tiles, block_rows, lanes)
        .transpose(0, 2, 1, 3)
        .reshape(rows, width)
    )


def on_device(
    frames, llm_grad, dest_rank, utt_lengths, valid, norm_gain, up_weight, kernel, down_weight
):
    rows, width = frames.shape
    n_data = lax.axis_size("dp")
    n_shard = lax.axis_size("fsdp")
    ranks = n_data * n_shard
    out_grad = route(llm_grad, dest_rank, ranks)
    up_full = lax.all_gather(up_weight, "fsdp", axis=0, tiled=True)
    down_full = lax.all_gather(down_weight, "fsdp", axis=0, tiled=True)
    taps = kernel.shape[0]
    middle = (taps - 1) // 2
    seg = segment_of(utt_lengths[0], rows)
    xf = frames.astype(jnp.float32)
    mean = jnp.mean(xf, axis=1, keepdims=True)
    var = jnp.mean((xf - mean) ** 2, axis=1, keepdims=True)
    rstd = lax.rsqrt(var + 1e-05)
    normed = (xf - mean) * rstd
    hidden = (normed * norm_gain[None, :]).astype(jnp.bfloat16)
    up = jnp.dot(hidden, up_full, preferred_element_type=jnp.float32)
    value = up[:, :width]
    sig_b = jax.nn.sigmoid(up[:, width:])
    glu = (value * sig_b).astype(jnp.bfloat16)
    glu_f = glu.astype(jnp.float32)
    keep = valid.astype(jnp.float32)[:, None]
    sames = []
    conv = jnp.zeros((rows, width), jnp.float32)
    for k in range(taps):
        offset = k - middle
        same = (shift_rows(seg, offset, -1) == seg).astype(jnp.float32)[:, None]
        sames.append(same)
        conv = conv + kernel[k][None, :] * shift_rows(glu_f, offset, 0.0) * same
    conv = conv * keep
    sig_c = jax.nn.sigmoid(conv)
    act = (conv * sig_c).astype(jnp.bfloat16)
    act_grad = jnp.dot(out_grad, down_full.T, preferred_element_type=jnp.float32)
    conv_grad = act_grad * sig_c * (1.0 + conv * (1.0 - sig_c)) * keep
    glu_grad = jnp.zeros((rows, width), jnp.float32)
    for k in range(taps):
        offset = k - middle
        glu_grad = glu_grad + kernel[k][None, :] * (
            shift_rows(conv_grad, -offset, 0.0) * sames[taps - 1 - k]
        )
    value_grad = glu_grad * sig_b
    gate_grad = glu_grad * value * sig_b * (1.0 - sig_b)
    up_out_grad = jnp.concatenate([value_grad, gate_grad], axis=1).astype(jnp.bfloat16)
    weight_terms = jnp.concatenate(
        [contract_rows(hidden, up_out_grad), contract_rows(act, out_grad)], axis=1
    ).astype(jnp.bfloat16)
    weight_terms, conv_grad, up_out_grad = lax.optimization_barrier(
        (weight_terms, conv_grad, up_out_grad)
    )
    shard_sum = lax.psum_scatter(weight_terms, "fsdp", scatter_dimension=0, tiled=True)
    kernel_rows = []
    for k in range(taps):
        offset = k - middle
        masked = conv_grad * sames[k]
        kernel_rows.append(jnp.sum(masked * shift_rows(glu_f, offset, 0.0), axis=0))
    kernel_term = jnp.stack(kernel_rows, axis=0)
    hidden_grad = jnp.dot(up_out_grad, up_full.T, preferred_element_type=jnp.float32)
    gain_term = jnp.sum(hidden_grad * normed, axis=0)
    scaled = hidden_grad * norm_gain[None, :]
    input_grad = rstd * (
        scaled
        - jnp.mean(scaled, axis=1, keepdims=True)
        - normed * jnp.mean(scaled * normed, axis=1, keepdims=True)
    )
    small = jnp.concatenate([kernel_term, gain_term[None, :]], axis=0)
    small = group_sum(group_sum(small, "fsdp"), "dp")
    shard_sum = butterfly(shard_sum.astype(jnp.float32), "dp")
    return (
        input_grad.astype(jnp.bfloat16),
        shard_sum[:, : 2 * width],
        shard_sum[:, 2 * width :],
        small[:taps],
        small[taps],
    )


def solution(mesh):
    return jax.shard_map(
        on_device,
        mesh=mesh,
        in_specs=(
            P(("dp", "fsdp"), None),
            P(("dp", "fsdp"), None),
            P(("dp", "fsdp"), None),
            P(("dp", "fsdp"), None),
            P(("dp", "fsdp")),
            P(),
            P("fsdp", None),
            P(),
            P("fsdp", None),
        ),
        out_specs=(P(("dp", "fsdp"), None), P("fsdp", None), P("fsdp", None), P(), P()),
        check_vma=False,
    )
```

```python
import jax
import jax.numpy as jnp
from jax import lax
from jax.sharding import PartitionSpec as P

CAPB = 1


def shift_rows(values, offset, fill):
    rows = values.shape[0]
    if offset == 0:
        return values
    pad = jnp.full((abs(offset),) + values.shape[1:], fill, values.dtype)
    if offset > 0:
        return jnp.concatenate([values[offset:], pad], axis=0)
    return jnp.concatenate([pad, values[: rows + offset]], axis=0)


def segment_of(lengths, rows):
    ends = jnp.cumsum(lengths)
    place = jnp.arange(rows, dtype=jnp.int32)
    return jnp.sum((place[:, None] >= ends[None, :]).astype(jnp.int32), axis=1)


def contract_rows(left, right):
    return lax.dot_general(
        left, right, (((0,), (0,)), ((), ())), preferred_element_type=jnp.float32
    )


def butterfly(x, axis):
    size = lax.axis_size(axis)
    if size & (size - 1):
        return lax.psum(x, axis)
    m = 1
    while m < size:
        x = x + lax.ppermute(x, axis, [(i, i ^ m) for i in range(size)])
        m *= 2
    return x


def group_sum(x, axis):
    size = lax.axis_size(axis)
    if size & (size - 1):
        return lax.psum(x, axis)
    bits = size.bit_length() - 1
    shift = 0
    me = lax.axis_index(axis)
    while shift < bits:
        width = 1 if (shift == 0 and bits % 2) else 2
        n = 1 << width
        got = [x] + [
            lax.ppermute(x, axis, [(i, i ^ (d << shift)) for i in range(size)]) for d in range(1, n)
        ]
        stack = jnp.stack(got)
        mine = (me >> shift) & (n - 1)
        total = stack[mine]
        for m in range(1, n):
            total = total + stack[m ^ mine]
        x = total
        shift += width
    return x


def route(llm_grad, dest_rank, ranks):
    rows, width = llm_grad.shape
    blocks_dev = dest_rank.shape[1]
    block_rows = rows // blocks_dev
    lanes = 128
    col_tiles = width // lanes
    body = block_rows * col_tiles
    targets = dest_rank[0]
    grad_tiles = (
        llm_grad.reshape(blocks_dev, block_rows, col_tiles, lanes)
        .transpose(0, 2, 1, 3)
        .reshape(blocks_dev, body, lanes)
    )
    tags = jnp.broadcast_to(
        (jnp.arange(blocks_dev, dtype=jnp.float32) + 1.0)[:, None, None], (blocks_dev, 16, lanes)
    ).astype(jnp.bfloat16)
    tagged = jnp.concatenate([grad_tiles, tags], axis=1)
    send_sel = (targets[None, :] == jnp.arange(ranks, dtype=jnp.int32)[:, None]).astype(jnp.bfloat16)
    outbox = jnp.einsum(
        "dj,jqc->dqc", send_sel, tagged, preferred_element_type=jnp.float32
    ).astype(jnp.bfloat16)
    inbox = lax.all_to_all(outbox, ("dp", "fsdp"), split_axis=0, concat_axis=0, tiled=True)
    tag_in = inbox[:, body, 0].astype(jnp.float32)
    recv_sel = (
        tag_in[None, :] == (jnp.arange(blocks_dev, dtype=jnp.float32) + 1.0)[:, None]
    ).astype(jnp.bfloat16)
    placed = jnp.einsum(
        "js,sqc->jqc", recv_sel, inbox[:, :body, :], preferred_element_type=jnp.float32
    ).astype(jnp.bfloat16)
    return (
        placed.reshape(blocks_dev, col_tiles, block_rows, lanes)
        .transpose(0, 2, 1, 3)
        .reshape(rows, width)
    )


def on_device(
    frames, llm_grad, dest_rank, utt_lengths, valid, norm_gain, up_weight, kernel, down_weight
):
    rows, width = frames.shape
    n_data = lax.axis_size("dp")
    n_shard = lax.axis_size("fsdp")
    ranks = n_data * n_shard
    out_grad = route(llm_grad, dest_rank, ranks)
    up_full = lax.all_gather(up_weight, "fsdp", axis=0, tiled=True)
    down_full = lax.all_gather(down_weight, "fsdp", axis=0, tiled=True)
    taps = kernel.shape[0]
    middle = (taps - 1) // 2
    seg = segment_of(utt_lengths[0], rows)
    xf = frames.astype(jnp.float32)
    mean = jnp.mean(xf, axis=1, keepdims=True)
    var = jnp.mean((xf - mean) ** 2, axis=1, keepdims=True)
    rstd = lax.rsqrt(var + 1e-05)
    normed = (xf - mean) * rstd
    hidden = (normed * norm_gain[None, :]).astype(jnp.bfloat16)
    up = jnp.dot(hidden, up_full, preferred_element_type=jnp.float32)
    value = up[:, :width]
    sig_b = jax.nn.sigmoid(up[:, width:])
    glu = (value * sig_b).astype(jnp.bfloat16)
    glu_f = glu.astype(jnp.float32)
    keep = valid.astype(jnp.float32)[:, None]
    sames = []
    conv = jnp.zeros((rows, width), jnp.float32)
    for k in range(taps):
        offset = k - middle
        same = (shift_rows(seg, offset, -1) == seg).astype(jnp.float32)[:, None]
        sames.append(same)
        conv = conv + kernel[k][None, :] * shift_rows(glu_f, offset, 0.0) * same
    conv = conv * keep
    sig_c = jax.nn.sigmoid(conv)
    act = (conv * sig_c).astype(jnp.bfloat16)
    conv_kept, sig_c_kept, value_kept, sig_b_kept = lax.optimization_barrier((conv, sig_c, value, sig_b))
    act_grad = jnp.dot(out_grad, down_full.T, preferred_element_type=jnp.float32)
    conv_grad = act_grad * sig_c_kept * (1.0 + conv_kept * (1.0 - sig_c_kept)) * keep
    glu_grad = jnp.zeros((rows, width), jnp.float32)
    for k in range(taps):
        offset = k - middle
        glu_grad = glu_grad + kernel[k][None, :] * (
            shift_rows(conv_grad, -offset, 0.0) * sames[taps - 1 - k]
        )
    value_grad = glu_grad * sig_b_kept
    gate_grad = glu_grad * value_kept * sig_b_kept * (1.0 - sig_b_kept)
    up_out_grad = jnp.concatenate([value_grad, gate_grad], axis=1).astype(jnp.bfloat16)
    weight_terms = jnp.concatenate(
        [contract_rows(hidden, up_out_grad), contract_rows(act, out_grad)], axis=1
    ).astype(jnp.bfloat16)
    weight_terms, conv_grad, up_out_grad = lax.optimization_barrier(
        (weight_terms, conv_grad, up_out_grad)
    )
    shard_sum = lax.psum_scatter(weight_terms, "fsdp", scatter_dimension=0, tiled=True)
    kernel_rows = []
    for k in range(taps):
        offset = k - middle
        masked = conv_grad * sames[k]
        kernel_rows.append(jnp.sum(masked * shift_rows(glu_f, offset, 0.0), axis=0))
    kernel_term = jnp.stack(kernel_rows, axis=0)
    hidden_grad = jnp.dot(up_out_grad, up_full.T, preferred_element_type=jnp.float32)
    gain_term = jnp.sum(hidden_grad * normed, axis=0)
    scaled = hidden_grad * norm_gain[None, :]
    input_grad = rstd * (
        scaled
        - jnp.mean(scaled, axis=1, keepdims=True)
        - normed * jnp.mean(scaled * normed, axis=1, keepdims=True)
    )
    small = jnp.concatenate([kernel_term, gain_term[None, :]], axis=0)
    small = group_sum(group_sum(small, "fsdp"), "dp")
    shard_sum = butterfly(shard_sum.astype(jnp.float32), "dp")
    return (
        input_grad.astype(jnp.bfloat16),
        shard_sum[:, : 2 * width],
        shard_sum[:, 2 * width :],
        small[:taps],
        small[taps],
    )


def solution(mesh):
    return jax.shard_map(
        on_device,
        mesh=mesh,
        in_specs=(
            P(("dp", "fsdp"), None),
            P(("dp", "fsdp"), None),
            P(("dp", "fsdp"), None),
            P(("dp", "fsdp"), None),
            P(("dp", "fsdp")),
            P(),
            P("fsdp", None),
            P(),
            P("fsdp", None),
        ),
        out_specs=(P(("dp", "fsdp"), None), P("fsdp", None), P("fsdp", None), P(), P()),
        check_vma=False,
    )
```

```python
import jax
import jax.numpy as jnp
from jax import lax
from jax.sharding import PartitionSpec as P

CAPB = 1


def shift_rows(values, offset, fill):
    rows = values.shape[0]
    if offset == 0:
        return values
    pad = jnp.full((abs(offset),) + values.shape[1:], fill, values.dtype)
    if offset > 0:
        return jnp.concatenate([values[offset:], pad], axis=0)
    return jnp.concatenate([pad, values[: rows + offset]], axis=0)


def segment_of(lengths, rows):
    ends = jnp.cumsum(lengths)
    place = jnp.arange(rows, dtype=jnp.int32)
    return jnp.sum((place[:, None] >= ends[None, :]).astype(jnp.int32), axis=1)


def contract_rows(left, right):
    return lax.dot_general(
        left, right, (((0,), (0,)), ((), ())), preferred_element_type=jnp.float32
    )


def butterfly(x, axis):
    size = lax.axis_size(axis)
    if size & (size - 1):
        return lax.psum(x, axis)
    m = 1
    while m < size:
        x = x + lax.ppermute(x, axis, [(i, i ^ m) for i in range(size)])
        m *= 2
    return x


def group_sum(x, axis):
    size = lax.axis_size(axis)
    if size & (size - 1):
        return lax.psum(x, axis)
    bits = size.bit_length() - 1
    shift = 0
    me = lax.axis_index(axis)
    while shift < bits:
        width = 1 if (shift == 0 and bits % 2) else 2
        n = 1 << width
        got = [x] + [
            lax.ppermute(x, axis, [(i, i ^ (d << shift)) for i in range(size)]) for d in range(1, n)
        ]
        stack = jnp.stack(got)
        mine = (me >> shift) & (n - 1)
        total = stack[mine]
        for m in range(1, n):
            total = total + stack[m ^ mine]
        x = total
        shift += width
    return x


def route(llm_grad, dest_rank, ranks):
    rows, width = llm_grad.shape
    blocks_dev = dest_rank.shape[1]
    block_rows = rows // blocks_dev
    lanes = 128
    col_tiles = width // lanes
    body = block_rows * col_tiles
    targets = dest_rank[0]
    grad_tiles = (
        llm_grad.reshape(blocks_dev, block_rows, col_tiles, lanes)
        .transpose(0, 2, 1, 3)
        .reshape(blocks_dev, body, lanes)
    )
    tags = jnp.broadcast_to(
        (jnp.arange(blocks_dev, dtype=jnp.float32) + 1.0)[:, None, None], (blocks_dev, 16, lanes)
    ).astype(jnp.bfloat16)
    tagged = jnp.concatenate([grad_tiles, tags], axis=1)
    send_sel = (targets[None, :] == jnp.arange(ranks, dtype=jnp.int32)[:, None]).astype(jnp.bfloat16)
    outbox = jnp.einsum(
        "dj,jqc->dqc", send_sel, tagged, preferred_element_type=jnp.float32
    ).astype(jnp.bfloat16)
    inbox = lax.all_to_all(outbox, ("dp", "fsdp"), split_axis=0, concat_axis=0, tiled=True)
    tag_in = inbox[:, body, 0].astype(jnp.float32)
    recv_sel = (
        tag_in[None, :] == (jnp.arange(blocks_dev, dtype=jnp.float32) + 1.0)[:, None]
    ).astype(jnp.bfloat16)
    placed = jnp.einsum(
        "js,sqc->jqc", recv_sel, inbox[:, :body, :], preferred_element_type=jnp.float32
    ).astype(jnp.bfloat16)
    return (
        placed.reshape(blocks_dev, col_tiles, block_rows, lanes)
        .transpose(0, 2, 1, 3)
        .reshape(rows, width)
    )


def on_device(
    frames, llm_grad, dest_rank, utt_lengths, valid, norm_gain, up_weight, kernel, down_weight
):
    rows, width = frames.shape
    n_data = lax.axis_size("dp")
    n_shard = lax.axis_size("fsdp")
    ranks = n_data * n_shard
    out_grad = route(llm_grad, dest_rank, ranks)
    up_full = lax.all_gather(up_weight, "fsdp", axis=0, tiled=True)
    down_full = lax.all_gather(down_weight, "fsdp", axis=0, tiled=True)
    taps = kernel.shape[0]
    middle = (taps - 1) // 2
    seg = segment_of(utt_lengths[0], rows)
    xf = frames.astype(jnp.float32)
    mean = jnp.mean(xf, axis=1, keepdims=True)
    var = jnp.mean((xf - mean) ** 2, axis=1, keepdims=True)
    rstd = lax.rsqrt(var + 1e-05)
    normed = (xf - mean) * rstd
    hidden = (normed * norm_gain[None, :]).astype(jnp.bfloat16)
    up = jnp.dot(hidden, up_full, preferred_element_type=jnp.float32)
    value = up[:, :width]
    sig_b = jax.nn.sigmoid(up[:, width:])
    glu = (value * sig_b).astype(jnp.bfloat16)
    glu_f = glu.astype(jnp.float32)
    keep = valid.astype(jnp.float32)[:, None]
    sames = []
    conv = jnp.zeros((rows, width), jnp.float32)
    for k in range(taps):
        offset = k - middle
        same = (shift_rows(seg, offset, -1) == seg).astype(jnp.float32)[:, None]
        sames.append(same)
        conv = conv + kernel[k][None, :] * shift_rows(glu_f, offset, 0.0) * same
    conv = conv * keep
    sig_c = jax.nn.sigmoid(conv)
    act = (conv * sig_c).astype(jnp.bfloat16)
    act_grad = jnp.dot(out_grad, down_full.T, preferred_element_type=jnp.float32)
    conv_grad = act_grad * sig_c * (1.0 + conv * (1.0 - sig_c)) * keep
    glu_grad = jnp.zeros((rows, width), jnp.float32)
    for k in range(taps):
        offset = k - middle
        glu_grad = glu_grad + kernel[k][None, :] * (
            shift_rows(conv_grad, -offset, 0.0) * sames[taps - 1 - k]
        )
    value_grad = glu_grad * sig_b
    gate_grad = glu_grad * value * sig_b * (1.0 - sig_b)
    up_out_grad = jnp.concatenate([value_grad, gate_grad], axis=1).astype(jnp.bfloat16)
    weight_terms = jnp.concatenate(
        [contract_rows(hidden, up_out_grad), contract_rows(act, out_grad)], axis=1
    ).astype(jnp.bfloat16)
    weight_terms, conv_grad, up_out_grad = lax.optimization_barrier(
        (weight_terms, conv_grad, up_out_grad)
    )
    shard_sum = lax.psum_scatter(weight_terms, "fsdp", scatter_dimension=0, tiled=True)
    kernel_rows = []
    for k in range(taps):
        offset = k - middle
        masked = conv_grad * sames[k]
        kernel_rows.append(jnp.sum(masked * shift_rows(glu_f, offset, 0.0), axis=0))
    kernel_term = jnp.stack(kernel_rows, axis=0)
    hidden_grad = jnp.dot(up_out_grad, up_full.T, preferred_element_type=jnp.float32)
    gain_term = jnp.sum(hidden_grad * normed, axis=0)
    scaled = hidden_grad * norm_gain[None, :]
    input_grad = rstd * (
        scaled
        - jnp.mean(scaled, axis=1, keepdims=True)
        - normed * jnp.mean(scaled * normed, axis=1, keepdims=True)
    )
    small = jnp.concatenate([kernel_term, gain_term[None, :]], axis=0)
    small = group_sum(group_sum(small, "fsdp"), "dp")
    n_dp = lax.axis_size("dp")
    if n_dp > 1 and not n_dp & (n_dp - 1):
        swap = [(i, i ^ 1) for i in range(n_dp)]
        shard_sum = shard_sum.astype(jnp.float32) + lax.ppermute(shard_sum, "dp", swap).astype(
            jnp.float32
        )
        m = 2
        while m < n_dp:
            shard_sum = shard_sum + lax.ppermute(shard_sum, "dp", [(i, i ^ m) for i in range(n_dp)])
            m *= 2
    else:
        shard_sum = butterfly(shard_sum.astype(jnp.float32), "dp")
    return (
        input_grad.astype(jnp.bfloat16),
        shard_sum[:, : 2 * width],
        shard_sum[:, 2 * width :],
        small[:taps],
        small[taps],
    )


def solution(mesh):
    return jax.shard_map(
        on_device,
        mesh=mesh,
        in_specs=(
            P(("dp", "fsdp"), None),
            P(("dp", "fsdp"), None),
            P(("dp", "fsdp"), None),
            P(("dp", "fsdp"), None),
            P(("dp", "fsdp")),
            P(),
            P("fsdp", None),
            P(),
            P("fsdp", None),
        ),
        out_specs=(P(("dp", "fsdp"), None), P("fsdp", None), P("fsdp", None), P(), P()),
        check_vma=False,
    )
```

```python
import jax
import jax.numpy as jnp
from jax import lax
from jax.sharding import PartitionSpec as P

CAPB = 1


def shift_rows(values, offset, fill):
    rows = values.shape[0]
    if offset == 0:
        return values
    pad = jnp.full((abs(offset),) + values.shape[1:], fill, values.dtype)
    if offset > 0:
        return jnp.concatenate([values[offset:], pad], axis=0)
    return jnp.concatenate([pad, values[: rows + offset]], axis=0)


def segment_of(lengths, rows):
    ends = jnp.cumsum(lengths)
    place = jnp.arange(rows, dtype=jnp.int32)
    return jnp.sum((place[:, None] >= ends[None, :]).astype(jnp.int32), axis=1)


def contract_rows(left, right):
    return lax.dot_general(
        left, right, (((0,), (0,)), ((), ())), preferred_element_type=jnp.float32
    )


def butterfly(x, axis):
    size = lax.axis_size(axis)
    if size & (size - 1):
        return lax.psum(x, axis)
    m = 1
    while m < size:
        x = x + lax.ppermute(x, axis, [(i, i ^ m) for i in range(size)])
        m *= 2
    return x


def group_sum(x, axis):
    size = lax.axis_size(axis)
    if size & (size - 1):
        return lax.psum(x, axis)
    bits = size.bit_length() - 1
    shift = 0
    me = lax.axis_index(axis)
    while shift < bits:
        width = 1 if (shift == 0 and bits % 2) else 2
        n = 1 << width
        got = [x] + [
            lax.ppermute(x, axis, [(i, i ^ (d << shift)) for i in range(size)]) for d in range(1, n)
        ]
        stack = jnp.stack(got)
        mine = (me >> shift) & (n - 1)
        total = stack[mine]
        for m in range(1, n):
            total = total + stack[m ^ mine]
        x = total
        shift += width
    return x


def route(llm_grad, dest_rank, ranks):
    rows, width = llm_grad.shape
    blocks_dev = dest_rank.shape[1]
    block_rows = rows // blocks_dev
    lanes = 128
    col_tiles = width // lanes
    body = block_rows * col_tiles
    targets = dest_rank[0]
    grad_tiles = (
        llm_grad.reshape(blocks_dev, block_rows, col_tiles, lanes)
        .transpose(0, 2, 1, 3)
        .reshape(blocks_dev, body, lanes)
    )
    tags = jnp.broadcast_to(
        (jnp.arange(blocks_dev, dtype=jnp.float32) + 1.0)[:, None, None], (blocks_dev, 16, lanes)
    ).astype(jnp.bfloat16)
    tagged = jnp.concatenate([grad_tiles, tags], axis=1)
    send_sel = (targets[None, :] == jnp.arange(ranks, dtype=jnp.int32)[:, None]).astype(jnp.bfloat16)
    outbox = jnp.einsum(
        "dj,jqc->dqc", send_sel, tagged, preferred_element_type=jnp.float32
    ).astype(jnp.bfloat16)
    inbox = lax.all_to_all(outbox, ("dp", "fsdp"), split_axis=0, concat_axis=0, tiled=True)
    tag_in = inbox[:, body, 0].astype(jnp.float32)
    recv_sel = (
        tag_in[None, :] == (jnp.arange(blocks_dev, dtype=jnp.float32) + 1.0)[:, None]
    ).astype(jnp.bfloat16)
    placed = jnp.einsum(
        "js,sqc->jqc", recv_sel, inbox[:, :body, :], preferred_element_type=jnp.float32
    ).astype(jnp.bfloat16)
    return (
        placed.reshape(blocks_dev, col_tiles, block_rows, lanes)
        .transpose(0, 2, 1, 3)
        .reshape(rows, width)
    )


def on_device(
    frames, llm_grad, dest_rank, utt_lengths, valid, norm_gain, up_weight, kernel, down_weight
):
    rows, width = frames.shape
    n_data = lax.axis_size("dp")
    n_shard = lax.axis_size("fsdp")
    ranks = n_data * n_shard
    out_grad = route(llm_grad, dest_rank, ranks)
    up_full = lax.all_gather(up_weight, "fsdp", axis=0, tiled=True)
    down_full = lax.all_gather(down_weight, "fsdp", axis=0, tiled=True)
    taps = kernel.shape[0]
    middle = (taps - 1) // 2
    seg = segment_of(utt_lengths[0], rows)
    xf = frames.astype(jnp.float32)
    mean = jnp.mean(xf, axis=1, keepdims=True)
    var = jnp.mean((xf - mean) ** 2, axis=1, keepdims=True)
    rstd = lax.rsqrt(var + 1e-05)
    normed = (xf - mean) * rstd
    hidden = (normed * norm_gain[None, :]).astype(jnp.bfloat16)
    up = jnp.dot(hidden, up_full, preferred_element_type=jnp.float32)
    value = up[:, :width]
    sig_b = jax.nn.sigmoid(up[:, width:])
    glu = (value * sig_b).astype(jnp.bfloat16)
    glu_f = glu.astype(jnp.float32)
    keep = valid.astype(jnp.float32)[:, None]
    sames = []
    conv = jnp.zeros((rows, width), jnp.float32)
    for k in range(taps):
        offset = k - middle
        same = (shift_rows(seg, offset, -1) == seg).astype(jnp.float32)[:, None]
        sames.append(same)
        conv = conv + kernel[k][None, :] * shift_rows(glu_f, offset, 0.0) * same
    conv = conv * keep
    sig_c = jax.nn.sigmoid(conv)
    act = (conv * sig_c).astype(jnp.bfloat16)
    act_grad = jnp.dot(out_grad, down_full.T, preferred_element_type=jnp.float32)
    conv_grad = act_grad * sig_c * (1.0 + conv * (1.0 - sig_c)) * keep
    glu_grad = jnp.zeros((rows, width), jnp.float32)
    for k in range(taps):
        offset = k - middle
        glu_grad = glu_grad + kernel[k][None, :] * (
            shift_rows(conv_grad, -offset, 0.0) * sames[taps - 1 - k]
        )
    value_grad = glu_grad * sig_b
    gate_grad = glu_grad * value * sig_b * (1.0 - sig_b)
    up_out_grad = jnp.concatenate([value_grad, gate_grad], axis=1).astype(jnp.bfloat16)
    weight_terms = jnp.concatenate(
        [contract_rows(hidden, up_out_grad), contract_rows(act, out_grad)], axis=1
    ).astype(jnp.bfloat16)
    weight_terms, conv_grad, up_out_grad = lax.optimization_barrier(
        (weight_terms, conv_grad, up_out_grad)
    )
    shard_sum = lax.psum_scatter(weight_terms, "fsdp", scatter_dimension=0, tiled=True)
    kernel_rows = []
    for k in range(taps):
        offset = k - middle
        masked = conv_grad * sames[k]
        kernel_rows.append(jnp.sum(masked * shift_rows(glu_f, offset, 0.0), axis=0))
    kernel_term = jnp.stack(kernel_rows, axis=0)
    hidden_grad = jnp.dot(up_out_grad, up_full.T, preferred_element_type=jnp.float32)
    gain_term = jnp.sum(hidden_grad * normed, axis=0)
    scaled = hidden_grad * norm_gain[None, :]
    input_grad = rstd * (
        scaled
        - jnp.mean(scaled, axis=1, keepdims=True)
        - normed * jnp.mean(scaled * normed, axis=1, keepdims=True)
    )
    small = jnp.concatenate([kernel_term, gain_term[None, :]], axis=0)
    small = group_sum(group_sum(small, "fsdp"), "dp")
    n_dp = lax.axis_size("dp")
    if n_dp > 1 and not n_dp & (n_dp - 1):
        swap = [(i, i ^ 1) for i in range(n_dp)]
        shard_sum = shard_sum.astype(jnp.float32) + lax.ppermute(shard_sum, "dp", swap).astype(
            jnp.float32
        )
        m = 2
        while m < n_dp:
            half = shard_sum.astype(jnp.bfloat16)
            shard_sum = half.astype(jnp.float32) + lax.ppermute(
                half, "dp", [(i, i ^ m) for i in range(n_dp)]
            ).astype(jnp.float32)
            m *= 2
    else:
        shard_sum = butterfly(shard_sum.astype(jnp.float32), "dp")
    return (
        input_grad.astype(jnp.bfloat16),
        shard_sum[:, : 2 * width],
        shard_sum[:, 2 * width :],
        small[:taps],
        small[taps],
    )


def solution(mesh):
    return jax.shard_map(
        on_device,
        mesh=mesh,
        in_specs=(
            P(("dp", "fsdp"), None),
            P(("dp", "fsdp"), None),
            P(("dp", "fsdp"), None),
            P(("dp", "fsdp"), None),
            P(("dp", "fsdp")),
            P(),
            P("fsdp", None),
            P(),
            P("fsdp", None),
        ),
        out_specs=(P(("dp", "fsdp"), None), P("fsdp", None), P("fsdp", None), P(), P()),
        check_vma=False,
    )
```

```python
import jax
import jax.numpy as jnp
from jax import lax
from jax.sharding import PartitionSpec as P

CAPB = 1


def shift_rows(values, offset, fill):
    rows = values.shape[0]
    if offset == 0:
        return values
    pad = jnp.full((abs(offset),) + values.shape[1:], fill, values.dtype)
    if offset > 0:
        return jnp.concatenate([values[offset:], pad], axis=0)
    return jnp.concatenate([pad, values[: rows + offset]], axis=0)


def segment_of(lengths, rows):
    ends = jnp.cumsum(lengths)
    place = jnp.arange(rows, dtype=jnp.int32)
    return jnp.sum((place[:, None] >= ends[None, :]).astype(jnp.int32), axis=1)


def contract_rows(left, right):
    return lax.dot_general(
        left, right, (((0,), (0,)), ((), ())), preferred_element_type=jnp.float32
    )


def butterfly(x, axis):
    size = lax.axis_size(axis)
    if size & (size - 1):
        return lax.psum(x, axis)
    m = 1
    while m < size:
        x = x + lax.ppermute(x, axis, [(i, i ^ m) for i in range(size)])
        m *= 2
    return x


def group_sum(x, axis):
    size = lax.axis_size(axis)
    if size & (size - 1):
        return lax.psum(x, axis)
    bits = size.bit_length() - 1
    shift = 0
    me = lax.axis_index(axis)
    while shift < bits:
        width = 1 if (shift == 0 and bits % 2) else 2
        n = 1 << width
        got = [x] + [
            lax.ppermute(x, axis, [(i, i ^ (d << shift)) for i in range(size)]) for d in range(1, n)
        ]
        stack = jnp.stack(got)
        mine = (me >> shift) & (n - 1)
        total = stack[mine]
        for m in range(1, n):
            total = total + stack[m ^ mine]
        x = total
        shift += width
    return x


def route(llm_grad, dest_rank, ranks):
    rows, width = llm_grad.shape
    blocks_dev = dest_rank.shape[1]
    block_rows = rows // blocks_dev
    lanes = 128
    col_tiles = width // lanes
    body = block_rows * col_tiles
    targets = dest_rank[0]
    grad_tiles = (
        llm_grad.reshape(blocks_dev, block_rows, col_tiles, lanes)
        .transpose(0, 2, 1, 3)
        .reshape(blocks_dev, body, lanes)
    )
    tags = jnp.broadcast_to(
        (jnp.arange(blocks_dev, dtype=jnp.float32) + 1.0)[:, None, None], (blocks_dev, 16, lanes)
    ).astype(jnp.bfloat16)
    tagged = jnp.concatenate([grad_tiles, tags], axis=1)
    send_sel = (targets[None, :] == jnp.arange(ranks, dtype=jnp.int32)[:, None]).astype(jnp.bfloat16)
    outbox = jnp.einsum(
        "dj,jqc->dqc", send_sel, tagged, preferred_element_type=jnp.float32
    ).astype(jnp.bfloat16)
    inbox = lax.all_to_all(outbox, ("dp", "fsdp"), split_axis=0, concat_axis=0, tiled=True)
    tag_in = inbox[:, body, 0].astype(jnp.float32)
    recv_sel = (
        tag_in[None, :] == (jnp.arange(blocks_dev, dtype=jnp.float32) + 1.0)[:, None]
    ).astype(jnp.bfloat16)
    placed = jnp.einsum(
        "js,sqc->jqc", recv_sel, inbox[:, :body, :], preferred_element_type=jnp.float32
    ).astype(jnp.bfloat16)
    return (
        placed.reshape(blocks_dev, col_tiles, block_rows, lanes)
        .transpose(0, 2, 1, 3)
        .reshape(rows, width)
    )


def on_device(
    frames, llm_grad, dest_rank, utt_lengths, valid, norm_gain, up_weight, kernel, down_weight
):
    rows, width = frames.shape
    n_data = lax.axis_size("dp")
    n_shard = lax.axis_size("fsdp")
    ranks = n_data * n_shard
    out_grad = route(llm_grad, dest_rank, ranks)
    up_full = lax.all_gather(up_weight, "fsdp", axis=0, tiled=True)
    down_full = lax.all_gather(down_weight, "fsdp", axis=0, tiled=True)
    taps = kernel.shape[0]
    middle = (taps - 1) // 2
    seg = segment_of(utt_lengths[0], rows)
    xf = frames.astype(jnp.float32)
    mean = jnp.mean(xf, axis=1, keepdims=True)
    var = jnp.mean((xf - mean) ** 2, axis=1, keepdims=True)
    rstd = lax.rsqrt(var + 1e-05)
    normed = (xf - mean) * rstd
    hidden = (normed * norm_gain[None, :]).astype(jnp.bfloat16)
    up = jnp.dot(hidden, up_full, preferred_element_type=jnp.float32)
    value = up[:, :width]
    sig_b = jax.nn.sigmoid(up[:, width:])
    glu = (value * sig_b).astype(jnp.bfloat16)
    glu_f = glu.astype(jnp.float32)
    keep = valid.astype(jnp.float32)[:, None]
    sames = []
    conv = jnp.zeros((rows, width), jnp.float32)
    for k in range(taps):
        offset = k - middle
        same = (shift_rows(seg, offset, -1) == seg).astype(jnp.float32)[:, None]
        sames.append(same)
        conv = conv + kernel[k][None, :] * shift_rows(glu_f, offset, 0.0) * same
    conv = conv * keep
    sig_c = jax.nn.sigmoid(conv)
    act = (conv * sig_c).astype(jnp.bfloat16)
    sig_b_kept = lax.optimization_barrier(sig_b)
    act_grad = jnp.dot(out_grad, down_full.T, preferred_element_type=jnp.float32)
    conv_grad = act_grad * sig_c * (1.0 + conv * (1.0 - sig_c)) * keep
    glu_grad = jnp.zeros((rows, width), jnp.float32)
    for k in range(taps):
        offset = k - middle
        glu_grad = glu_grad + kernel[k][None, :] * (
            shift_rows(conv_grad, -offset, 0.0) * sames[taps - 1 - k]
        )
    value_grad = glu_grad * sig_b_kept
    gate_grad = glu_grad * value * sig_b_kept * (1.0 - sig_b_kept)
    up_out_grad = jnp.concatenate([value_grad, gate_grad], axis=1).astype(jnp.bfloat16)
    weight_terms = jnp.concatenate(
        [contract_rows(hidden, up_out_grad), contract_rows(act, out_grad)], axis=1
    ).astype(jnp.bfloat16)
    weight_terms, conv_grad, up_out_grad = lax.optimization_barrier(
        (weight_terms, conv_grad, up_out_grad)
    )
    shard_sum = lax.psum_scatter(weight_terms, "fsdp", scatter_dimension=0, tiled=True)
    kernel_rows = []
    for k in range(taps):
        offset = k - middle
        masked = conv_grad * sames[k]
        kernel_rows.append(jnp.sum(masked * shift_rows(glu_f, offset, 0.0), axis=0))
    kernel_term = jnp.stack(kernel_rows, axis=0)
    hidden_grad = jnp.dot(up_out_grad, up_full.T, preferred_element_type=jnp.float32)
    gain_term = jnp.sum(hidden_grad * normed, axis=0)
    scaled = hidden_grad * norm_gain[None, :]
    input_grad = rstd * (
        scaled
        - jnp.mean(scaled, axis=1, keepdims=True)
        - normed * jnp.mean(scaled * normed, axis=1, keepdims=True)
    )
    small = jnp.concatenate([kernel_term, gain_term[None, :]], axis=0)
    small = group_sum(group_sum(small, "fsdp"), "dp")
    n_dp = lax.axis_size("dp")
    if n_dp > 1 and not n_dp & (n_dp - 1):
        swap = [(i, i ^ 1) for i in range(n_dp)]
        shard_sum = shard_sum.astype(jnp.float32) + lax.ppermute(shard_sum, "dp", swap).astype(
            jnp.float32
        )
        m = 2
        while m < n_dp:
            half = shard_sum.astype(jnp.bfloat16)
            shard_sum = half.astype(jnp.float32) + lax.ppermute(
                half, "dp", [(i, i ^ m) for i in range(n_dp)]
            ).astype(jnp.float32)
            m *= 2
    else:
        shard_sum = butterfly(shard_sum.astype(jnp.float32), "dp")
    return (
        input_grad.astype(jnp.bfloat16),
        shard_sum[:, : 2 * width],
        shard_sum[:, 2 * width :],
        small[:taps],
        small[taps],
    )


def solution(mesh):
    return jax.shard_map(
        on_device,
        mesh=mesh,
        in_specs=(
            P(("dp", "fsdp"), None),
            P(("dp", "fsdp"), None),
            P(("dp", "fsdp"), None),
            P(("dp", "fsdp"), None),
            P(("dp", "fsdp")),
            P(),
            P("fsdp", None),
            P(),
            P("fsdp", None),
        ),
        out_specs=(P(("dp", "fsdp"), None), P("fsdp", None), P("fsdp", None), P(), P()),
        check_vma=False,
    )
```
